256 devices in a mesh: rows: 32 (over y, z), grp: 8 (over x, core).
Axes of the slice: x: 4, y: 4, z: 8, core: 2. Of those that a mesh axis runs over, the one named last changes fastest.
Arguments:
- item_table: bfloat16 [507904, 128], P(('rows', 'grp'))
- histories: int32 [16384, 64], P(('rows', 'grp')), may hold values from 0 to 507903, as said below
- counts: int32 [16384], P(('rows', 'grp')), may hold values from 32 to 64
Outputs:
- user_vectors: float32 [16384, 128], P(('rows', 'grp'))
- item_rhs: float32 [507904, 128], P(('rows', 'grp'))
The draws below stay inside these ranges and needn't reach their ends.
Inputs may be any that keep to these rules, and one draw needn't show every extreme that they name: `histories`: entry j of user u is used only if j < counts[u]. The used entries of the users of one device name items of one owner (rows o * 1984 to (o + 1) * 1984 - 1) at most 32 times, and in every draw some owner is named exactly 32 times by the used entries of every device.
All inputs are finite; a program needn't handle non-finite values.
Results may differ from the reference program's by a relative error of at most 0.0064.
Values may be sent and summed in bfloat16 or wider, within the bound.
No kernel may reach another device: no remote copies, remote signals or barrier semaphores. Data moves between devices by JAX's collectives and lax.ppermute only.
A program may use at most 64 MiB of HBM per device.

```python
import jax
import jax.numpy as jnp
from jax import lax

K = 128
ITEM_DEV = 1984
U_DEV = 64
L = 64
ITERS = 3
ITEMS = 507904
USERS = 16384
CAP = 32


def history_layout(base_key):
    devices = ITEMS // ITEM_DEV
    lookups = U_DEV * L
    keys = jax.random.split(jax.random.fold_in(base_key, 7), 7)
    user_counts = jax.random.randint(keys[0], (devices, U_DEV), L // 2, L + 1)
    full_user = jax.random.randint(keys[1], (devices,), 0, U_DEV)
    user_counts = jnp.where(jnp.arange(U_DEV)[None, :] == full_user[:, None], L, user_counts)
    positions = jnp.arange(L)[None, None, :]
    live = (positions < user_counts[:, :, None]).reshape(devices, lookups)
    shuffles = jax.vmap(lambda subkey: jax.random.permutation(subkey, lookups))(jax.random.split(keys[2], devices))
    order_key = jnp.where(live, 0, lookups) + shuffles
    ranks = jnp.argsort(jnp.argsort(order_key, axis=1), axis=1)
    busiest = jax.random.randint(keys[3], (), 0, devices)
    owner_shuffles = jax.vmap(lambda subkey: jax.random.permutation(subkey, devices))(jax.random.split(keys[4], devices))
    owner_order = (owner_shuffles - owner_shuffles[:, :1] + busiest) % devices
    loads = jax.random.randint(keys[5], (devices, devices), CAP // 2, CAP + 1)
    loads = loads.at[:, 0].set(CAP)
    bounds = jnp.cumsum(loads, axis=1)
    places = jax.vmap(lambda edges, where: jnp.searchsorted(edges, where, side='right'))(bounds, ranks)
    places = jnp.minimum(places, devices - 1)
    owners = jnp.take_along_axis(owner_order, places, axis=1)
    local_rows = jax.random.randint(keys[6], (devices, lookups), 0, ITEM_DEV)
    item_ids = (owners * ITEM_DEV + local_rows).reshape(USERS, L)
    return (item_ids.astype(jnp.int32), user_counts.reshape(USERS).astype(jnp.int32))


def draw_histories(key, part):
    item_ids, user_counts = history_layout(key)
    return item_ids


def draw_counts(key, part):
    item_ids, user_counts = history_layout(key)
    return user_counts


def draw_item_table(key, part):
    keys = jax.random.split(jax.random.fold_in(key, 11), 3)
    fraction = jnp.arange(ITEMS, dtype=jnp.float32) / ITEMS
    rising = 1.0 + 2.0 * fraction
    row_scale = 10.0 ** jax.random.uniform(keys[0], (ITEMS,), jnp.float32)
    noise = jax.random.normal(keys[2], (ITEMS, K), jnp.float32)
    column_scale = 10.0 ** (0.5 * jax.random.uniform(keys[1], (K,), jnp.float32))
    values = 0.0045 * noise * (row_scale * rising)[:, None] * column_scale[None, :]
    return values.astype(jnp.bfloat16)


def setup_inputs(seed: int = 0) -> dict:
    streams_of = jax.random.split(jax.random.key(seed), 4)
    item_table = draw_item_table(jax.random.fold_in(streams_of[3], 71), 0)
    histories = draw_histories(jax.random.fold_in(streams_of[3], 71), 0)
    counts = draw_counts(jax.random.fold_in(streams_of[3], 71), 0)
    return {"item_table": item_table, "histories": histories, "counts": counts}


unobserved_weight = 25.0
ridge = 0.1


def rounded(values):
    narrow = values.astype(jnp.bfloat16)
    narrow = lax.optimization_barrier(narrow)
    return narrow.astype(jnp.float32)


def reference(item_table, histories, counts):
    embed_width = item_table.shape[1]
    highest = lax.Precision.HIGHEST
    table_blocks = item_table.reshape(ITEMS // ITEM_DEV, ITEM_DEV, embed_width)

    def add_gram(running, table_block):
        widened = table_block.astype(jnp.float32)
        return running + jnp.dot(widened.T, widened, precision=highest), None

    gramian, unused = lax.scan(add_gram, jnp.zeros((embed_width, embed_width), jnp.float32), table_blocks)
    unseen_scale = unobserved_weight / ITEMS
    user_ids = histories.reshape(USERS // U_DEV, U_DEV, L)
    user_counts = counts.reshape(USERS // U_DEV, U_DEV)

    def solve_block(item_rhs, inputs):
        id_block, count_block = inputs
        fetched = item_table[id_block].astype(jnp.float32)
        positions = jnp.arange(L).astype(jnp.int32)
        weights = (positions[None, :] < count_block[:, None]).astype(jnp.float32)
        target = jnp.einsum("ul,ulk->uk", weights, fetched, precision=highest)

        def operate(direction):
            narrow = rounded(direction)
            scores = jnp.einsum("ulk,uk->ul", fetched, narrow, precision=highest)
            scores = rounded(scores * weights)
            returned = jnp.einsum("ulk,ul->uk", fetched, scores, precision=highest)
            return unseen_scale * jnp.dot(direction, gramian, precision=highest) + returned + ridge * direction

        solution = jnp.zeros_like(target)
        residual = target
        direction = target
        norm_now = jnp.sum(residual * residual, axis=1)
        for iteration in range(ITERS):
            applied = operate(direction)
            step_size = norm_now / jnp.sum(direction * applied, axis=1)
            solution = solution + step_size[:, None] * direction
            residual = residual - step_size[:, None] * applied
            norm_next = jnp.sum(residual * residual, axis=1)
            direction = residual + (norm_next / norm_now)[:, None] * direction
            norm_now = norm_next
        spread = solution[:, None, :] * weights[:, :, None]
        item_rhs = item_rhs.at[id_block.reshape(-1)].add(spread.reshape(-1, embed_width))
        return item_rhs, solution

    item_rhs, solutions = lax.scan(solve_block, jnp.zeros((ITEMS, embed_width), jnp.float32), (user_ids, user_counts))
    return solutions.reshape(USERS, embed_width), item_rhs
```

```python
import jax
import jax.numpy as jnp
from jax import lax
from jax.sharding import PartitionSpec as P

ITERS = 3


unobserved_weight = 25.0
ridge = 0.1


def exchange(values):
    return lax.all_to_all(values, ("rows", "grp"), 0, 0, tiled=True)


def sum_over_devices(value):
    for axis in ("grp", "rows"):
        size = lax.axis_size(axis)
        stride = 1
        while stride < size:
            partners = [(i, i ^ stride) for i in range(size)]
            value = value + lax.ppermute(value, axis, partners)
            stride *= 2
    return value


def on_device(item_table, histories, counts):
    row_count = lax.axis_size("rows")
    group_count = lax.axis_size("grp")
    devices = row_count * group_count
    table_rows, embed_width = item_table.shape
    user_count, history_length = histories.shape
    lookups = user_count * history_length
    capacity = max(4, 2 * lookups // devices)
    slots_total = devices * capacity
    bf16 = jnp.bfloat16
    f32 = jnp.float32

    local_gram = lax.dot_general(
        item_table, item_table, (((0,), (0,)), ((), ())), preferred_element_type=f32
    )
    gramian = sum_over_devices(local_gram)

    positions = lax.broadcasted_iota(jnp.int32, (user_count, history_length), 1)
    live = positions < counts[:, None]
    owners = histories // table_rows
    local_rows = histories - owners * table_rows
    owner_ids = lax.broadcasted_iota(jnp.int32, (user_count, history_length, devices), 2)
    by_owner = ((owners[:, :, None] == owner_ids) & live[:, :, None]).astype(bf16)
    slot_ids = lax.broadcasted_iota(jnp.int32, (history_length, history_length), 0)
    earlier = (lax.broadcasted_iota(jnp.int32, (history_length, history_length), 1) < slot_ids).astype(bf16)
    within_user = jnp.einsum("jk,uko->ujo", earlier, by_owner, preferred_element_type=f32)
    per_user = jnp.sum(by_owner.astype(f32), axis=1)
    user_ids = lax.broadcasted_iota(jnp.int32, (user_count, user_count), 0)
    earlier_users = (lax.broadcasted_iota(jnp.int32, (user_count, user_count), 1) < user_ids).astype(bf16)
    before_user = jnp.einsum("uv,vo->uo", earlier_users, per_user.astype(bf16), preferred_element_type=f32)
    ranks = jnp.sum(by_owner.astype(f32) * (within_user + before_user[:, None, :]), axis=2)
    rank_ids = lax.broadcasted_iota(jnp.int32, (user_count, history_length, capacity), 2)
    by_rank = ((ranks.astype(jnp.int32)[:, :, None] == rank_ids) & live[:, :, None]).astype(bf16)

    row_high = local_rows // 32
    row_low = local_rows - row_high * 32
    user_of = lax.broadcasted_iota(jnp.int32, (user_count, history_length), 0)
    payload = jnp.stack([row_high, row_low, user_of, jnp.ones_like(user_of)], axis=2).astype(bf16)
    spread = (payload[:, :, :, None] * by_rank[:, :, None, :]).reshape(lookups, 4 * capacity)
    slots = jnp.einsum(
        "io,ic->oc", by_owner.reshape(lookups, devices), spread, preferred_element_type=f32
    ).reshape(devices, 4, capacity)
    slots = slots.astype(jnp.int32)
    requests = slots[:, 0] * 32 + slots[:, 1]
    slot_user = slots[:, 2].reshape(slots_total)
    slot_used = slots[:, 3].reshape(slots_total)

    slot_index = (owners * capacity + ranks.astype(jnp.int32)).reshape(lookups)

    incoming = exchange(requests).reshape(slots_total)
    answered = jnp.take(item_table, incoming, axis=0, mode="clip")
    reply_rows = exchange(answered.reshape(devices, capacity, embed_width)).reshape(
        slots_total, embed_width
    )
    fetched = jnp.take(reply_rows, slot_index, axis=0, mode="clip").reshape(
        user_count, history_length, embed_width
    )
    weights = live.astype(f32)
    narrow_weights = weights.astype(bf16)
    target = jnp.einsum("ul,ulk->uk", narrow_weights, fetched, preferred_element_type=f32)
    unseen_scale = unobserved_weight / (table_rows * devices)
    solution = jnp.zeros_like(target)
    residual = target
    direction = target
    norm_now = jnp.sum(residual * residual, axis=1)
    for iteration in range(ITERS):
        narrow = direction.astype(bf16)
        scores = jnp.einsum("ulk,uk->ul", fetched, narrow, preferred_element_type=f32)
        scores = (scores * weights).astype(bf16)
        returned = jnp.einsum("ulk,ul->uk", fetched, scores, preferred_element_type=f32)
        curved = jnp.dot(direction, gramian, precision=lax.Precision.HIGHEST)
        applied = unseen_scale * curved + returned + ridge * direction
        step_size = norm_now / jnp.sum(direction * applied, axis=1)
        solution = solution + step_size[:, None] * direction
        residual = residual - step_size[:, None] * applied
        norm_next = jnp.sum(residual * residual, axis=1)
        direction = residual + (norm_next / norm_now)[:, None] * direction
        norm_now = norm_next

    member_ids = lax.broadcasted_iota(jnp.int32, (slots_total, user_count), 1)
    member = ((slot_user[:, None] == member_ids) & (slot_used[:, None] > 0)).astype(bf16)
    partials = jnp.einsum("su,uk->sk", member, solution.astype(bf16), preferred_element_type=f32)
    partials = partials.astype(bf16).reshape(devices, capacity, embed_width)
    arrived = exchange(partials).reshape(slots_total, embed_width)
    item_rhs = (
        jnp.zeros((table_rows, embed_width), f32)
        .at[incoming]
        .add(arrived.astype(f32), mode="drop")
    )
    return (solution, item_rhs)


def solution(mesh):
    return jax.shard_map(
        on_device,
        mesh=mesh,
        in_specs=(P(("rows", "grp"), None), P(("rows", "grp"), None), P(("rows", "grp"))),
        out_specs=(P(("rows", "grp"), None), P(("rows", "grp"), None)),
        check_vma=False,
    )
```

```python
import jax
import jax.numpy as jnp
from jax import lax
from jax.sharding import PartitionSpec as P

ITERS = 3


unobserved_weight = 25.0
ridge = 0.1


def exchange(values):
    return lax.all_to_all(values, ("rows", "grp"), 0, 0, tiled=True)


def sum_over_devices(value):
    for axis in ("grp", "rows"):
        size = lax.axis_size(axis)
        stride = 1
        while stride < size:
            partners = [(i, i ^ stride) for i in range(size)]
            value = value + lax.ppermute(value, axis, partners)
            stride *= 2
    return value


def on_device(item_table, histories, counts):
    row_count = lax.axis_size("rows")
    group_count = lax.axis_size("grp")
    devices = row_count * group_count
    table_rows, embed_width = item_table.shape
    user_count, history_length = histories.shape
    lookups = user_count * history_length
    capacity = max(4, 2 * lookups // devices)
    slots_total = devices * capacity
    bf16 = jnp.bfloat16
    f32 = jnp.float32

    local_gram = lax.dot_general(
        item_table, item_table, (((0,), (0,)), ((), ())), preferred_element_type=f32
    )
    gramian = sum_over_devices(local_gram)

    positions = lax.broadcasted_iota(jnp.int32, (user_count, history_length), 1)
    live = positions < counts[:, None]
    owners = histories // table_rows
    local_rows = histories - owners * table_rows
    owner_ids = lax.broadcasted_iota(jnp.int32, (user_count, history_length, devices), 2)
    by_owner = ((owners[:, :, None] == owner_ids) & live[:, :, None]).astype(bf16)
    slot_ids = lax.broadcasted_iota(jnp.int32, (history_length, history_length), 0)
    earlier = (lax.broadcasted_iota(jnp.int32, (history_length, history_length), 1) < slot_ids).astype(bf16)
    within_user = jnp.einsum("jk,uko->ujo", earlier, by_owner, preferred_element_type=f32)
    per_user = jnp.sum(by_owner.astype(f32), axis=1)
    user_ids = lax.broadcasted_iota(jnp.int32, (user_count, user_count), 0)
    earlier_users = (lax.broadcasted_iota(jnp.int32, (user_count, user_count), 1) < user_ids).astype(bf16)
    before_user = jnp.einsum("uv,vo->uo", earlier_users, per_user.astype(bf16), preferred_element_type=f32)
    ranks = jnp.sum(by_owner.astype(f32) * (within_user + before_user[:, None, :]), axis=2)
    rank_ids = lax.broadcasted_iota(jnp.int32, (user_count, history_length, capacity), 2)
    by_rank = ((ranks.astype(jnp.int32)[:, :, None] == rank_ids) & live[:, :, None]).astype(bf16)

    row_high = local_rows // 32
    row_low = local_rows - row_high * 32
    user_of = lax.broadcasted_iota(jnp.int32, (user_count, history_length), 0)
    payload = jnp.stack([row_high, row_low, user_of, jnp.ones_like(user_of)], axis=2).astype(bf16)
    spread = (payload[:, :, :, None] * by_rank[:, :, None, :]).reshape(lookups, 4 * capacity)
    slots = jnp.einsum(
        "io,ic->oc", by_owner.reshape(lookups, devices), spread, preferred_element_type=f32
    ).reshape(devices, 4, capacity)
    slots = slots.astype(jnp.int32)
    requests = slots[:, 0] * 32 + slots[:, 1]
    slot_user = slots[:, 2].reshape(slots_total)
    slot_used = slots[:, 3].reshape(slots_total)

    slot_index = (owners * capacity + ranks.astype(jnp.int32)).reshape(lookups)

    incoming = exchange(requests).reshape(slots_total)
    table_ids = lax.broadcasted_iota(jnp.int32, (slots_total, table_rows), 1)
    picks = (incoming[:, None] == table_ids).astype(bf16)
    answered = jnp.dot(picks, item_table, preferred_element_type=f32).astype(bf16)
    reply_rows = exchange(answered.reshape(devices, capacity, embed_width)).reshape(
        slots_total, embed_width
    )
    fetched = jnp.take(reply_rows, slot_index, axis=0, mode="clip").reshape(
        user_count, history_length, embed_width
    )
    weights = live.astype(f32)
    narrow_weights = weights.astype(bf16)
    target = jnp.einsum("ul,ulk->uk", narrow_weights, fetched, preferred_element_type=f32)
    unseen_scale = unobserved_weight / (table_rows * devices)
    solution = jnp.zeros_like(target)
    residual = target
    direction = target
    norm_now = jnp.sum(residual * residual, axis=1)
    for iteration in range(ITERS):
        narrow = direction.astype(bf16)
        scores = jnp.einsum("ulk,uk->ul", fetched, narrow, preferred_element_type=f32)
        scores = (scores * weights).astype(bf16)
        returned = jnp.einsum("ulk,ul->uk", fetched, scores, preferred_element_type=f32)
        curved = jnp.dot(direction, gramian, precision=lax.Precision.HIGHEST)
        applied = unseen_scale * curved + returned + ridge * direction
        step_size = norm_now / jnp.sum(direction * applied, axis=1)
        solution = solution + step_size[:, None] * direction
        residual = residual - step_size[:, None] * applied
        norm_next = jnp.sum(residual * residual, axis=1)
        direction = residual + (norm_next / norm_now)[:, None] * direction
        norm_now = norm_next

    member_ids = lax.broadcasted_iota(jnp.int32, (slots_total, user_count), 1)
    member = ((slot_user[:, None] == member_ids) & (slot_used[:, None] > 0)).astype(bf16)
    partials = jnp.einsum("su,uk->sk", member, solution.astype(bf16), preferred_element_type=f32)
    partials = partials.astype(bf16).reshape(devices, capacity, embed_width)
    arrived = exchange(partials).reshape(slots_total, embed_width)
    item_rhs = jnp.einsum("st,sk->tk", picks, arrived, preferred_element_type=f32)
    return (solution, item_rhs)


def solution(mesh):
    return jax.shard_map(
        on_device,
        mesh=mesh,
        in_specs=(P(("rows", "grp"), None), P(("rows", "grp"), None), P(("rows", "grp"))),
        out_specs=(P(("rows", "grp"), None), P(("rows", "grp"), None)),
        check_vma=False,
    )
```

```python
import jax
import jax.numpy as jnp
from jax import lax
from jax.experimental import pallas as pl
from jax.sharding import PartitionSpec as P

ITERS = 3


unobserved_weight = 25.0
ridge = 0.1


def exchange(values):
    return lax.all_to_all(values, ("rows", "grp"), 0, 0, tiled=True)


def sum_over_devices(value):
    for axis in ("grp", "rows"):
        size = lax.axis_size(axis)
        stride = 1
        while stride < size:
            partners = [(i, i ^ stride) for i in range(size)]
            value = value + lax.ppermute(value, axis, partners)
            stride *= 2
    return value


def pick_rows_kernel(index_ref, table_ref, out_ref):
    block = index_ref.shape[0]
    row_ids = lax.broadcasted_iota(jnp.int32, (block, table_ref.shape[0]), 1)
    picks = (index_ref[...] == row_ids).astype(jnp.bfloat16)
    out_ref[...] = jnp.dot(picks, table_ref[...], preferred_element_type=jnp.float32).astype(
        out_ref.dtype
    )


def pick_rows(table, index, block=512):
    count = index.shape[0]
    rows, width = table.shape
    padded = -(-rows // 256) * 256
    table = jnp.pad(table, ((0, padded - rows), (0, 0)))
    return pl.pallas_call(
        pick_rows_kernel,
        grid=(count // block,),
        in_specs=[
            pl.BlockSpec((block, 1), lambda i: (i, 0)),
            pl.BlockSpec((padded, width), lambda i: (0, 0)),
        ],
        out_specs=pl.BlockSpec((block, width), lambda i: (i, 0)),
        out_shape=jax.ShapeDtypeStruct((count, width), table.dtype),
    )(index.reshape(count, 1), table)


def add_rows_kernel(index_ref, values_ref, out_ref):
    @pl.when(pl.program_id(0) == 0)
    def _():
        out_ref[...] = jnp.zeros_like(out_ref)

    row_ids = lax.broadcasted_iota(jnp.int32, (out_ref.shape[0], index_ref.shape[1]), 0)
    picks = (row_ids == index_ref[...]).astype(jnp.bfloat16)
    out_ref[...] += jnp.dot(picks, values_ref[...], preferred_element_type=jnp.float32)


def add_rows(values, index, rows, block=512):
    count, width = values.shape
    return pl.pallas_call(
        add_rows_kernel,
        grid=(count // block,),
        in_specs=[
            pl.BlockSpec((1, block), lambda i: (0, i)),
            pl.BlockSpec((block, width), lambda i: (i, 0)),
        ],
        out_specs=pl.BlockSpec((rows, width), lambda i: (0, 0)),
        out_shape=jax.ShapeDtypeStruct((rows, width), jnp.float32),
    )(index.reshape(1, count), values)


def on_device(item_table, histories, counts):
    row_count = lax.axis_size("rows")
    group_count = lax.axis_size("grp")
    devices = row_count * group_count
    table_rows, embed_width = item_table.shape
    user_count, history_length = histories.shape
    lookups = user_count * history_length
    capacity = max(4, 2 * lookups // devices)
    slots_total = devices * capacity
    bf16 = jnp.bfloat16
    f32 = jnp.float32

    local_gram = lax.dot_general(
        item_table, item_table, (((0,), (0,)), ((), ())), preferred_element_type=f32
    )
    gramian = sum_over_devices(local_gram)

    positions = lax.broadcasted_iota(jnp.int32, (user_count, history_length), 1)
    live = positions < counts[:, None]
    owners = histories // table_rows
    local_rows = histories - owners * table_rows
    owner_ids = lax.broadcasted_iota(jnp.int32, (user_count, history_length, devices), 2)
    by_owner = ((owners[:, :, None] == owner_ids) & live[:, :, None]).astype(bf16)
    slot_ids = lax.broadcasted_iota(jnp.int32, (history_length, history_length), 0)
    earlier = (lax.broadcasted_iota(jnp.int32, (history_length, history_length), 1) < slot_ids).astype(bf16)
    within_user = jnp.einsum("jk,uko->ujo", earlier, by_owner, preferred_element_type=f32)
    per_user = jnp.sum(by_owner.astype(f32), axis=1)
    user_ids = lax.broadcasted_iota(jnp.int32, (user_count, user_count), 0)
    earlier_users = (lax.broadcasted_iota(jnp.int32, (user_count, user_count), 1) < user_ids).astype(bf16)
    before_user = jnp.einsum("uv,vo->uo", earlier_users, per_user.astype(bf16), preferred_element_type=f32)
    ranks = jnp.sum(by_owner.astype(f32) * (within_user + before_user[:, None, :]), axis=2)
    rank_ids = lax.broadcasted_iota(jnp.int32, (user_count, history_length, capacity), 2)
    by_rank = ((ranks.astype(jnp.int32)[:, :, None] == rank_ids) & live[:, :, None]).astype(bf16)

    row_high = local_rows // 32
    row_low = local_rows - row_high * 32
    user_of = lax.broadcasted_iota(jnp.int32, (user_count, history_length), 0)
    payload = jnp.stack([row_high, row_low, user_of, jnp.ones_like(user_of)], axis=2).astype(bf16)
    spread = (payload[:, :, :, None] * by_rank[:, :, None, :]).reshape(lookups, 4 * capacity)
    slots = jnp.einsum(
        "io,ic->oc", by_owner.reshape(lookups, devices), spread, preferred_element_type=f32
    ).reshape(devices, 4, capacity)
    slots = slots.astype(jnp.int32)
    requests = slots[:, 0] * 32 + slots[:, 1]
    slot_user = slots[:, 2].reshape(slots_total)
    slot_used = slots[:, 3].reshape(slots_total)

    slot_index = (owners * capacity + ranks.astype(jnp.int32)).reshape(lookups)

    incoming = exchange(requests).reshape(slots_total)
    answered = pick_rows(item_table, incoming)
    reply_rows = exchange(answered.reshape(devices, capacity, embed_width)).reshape(
        slots_total, embed_width
    )
    fetched = jnp.take(reply_rows, slot_index, axis=0, mode="clip").reshape(
        user_count, history_length, embed_width
    )
    weights = live.astype(f32)
    narrow_weights = weights.astype(bf16)
    target = jnp.einsum("ul,ulk->uk", narrow_weights, fetched, preferred_element_type=f32)
    unseen_scale = unobserved_weight / (table_rows * devices)
    solution = jnp.zeros_like(target)
    residual = target
    direction = target
    norm_now = jnp.sum(residual * residual, axis=1)
    for iteration in range(ITERS):
        narrow = direction.astype(bf16)
        scores = jnp.einsum("ulk,uk->ul", fetched, narrow, preferred_element_type=f32)
        scores = (scores * weights).astype(bf16)
        returned = jnp.einsum("ulk,ul->uk", fetched, scores, preferred_element_type=f32)
        curved = jnp.dot(direction, gramian, precision=lax.Precision.HIGHEST)
        applied = unseen_scale * curved + returned + ridge * direction
        step_size = norm_now / jnp.sum(direction * applied, axis=1)
        solution = solution + step_size[:, None] * direction
        residual = residual - step_size[:, None] * applied
        norm_next = jnp.sum(residual * residual, axis=1)
        direction = residual + (norm_next / norm_now)[:, None] * direction
        norm_now = norm_next

    member_ids = lax.broadcasted_iota(jnp.int32, (slots_total, user_count), 1)
    member = ((slot_user[:, None] == member_ids) & (slot_used[:, None] > 0)).astype(bf16)
    partials = jnp.einsum("su,uk->sk", member, solution.astype(bf16), preferred_element_type=f32)
    partials = partials.astype(bf16).reshape(devices, capacity, embed_width)
    arrived = exchange(partials).reshape(slots_total, embed_width)
    item_rhs = add_rows(arrived, incoming, table_rows)
    return (solution, item_rhs)


def solution(mesh):
    return jax.shard_map(
        on_device,
        mesh=mesh,
        in_specs=(P(("rows", "grp"), None), P(("rows", "grp"), None), P(("rows", "grp"))),
        out_specs=(P(("rows", "grp"), None), P(("rows", "grp"), None)),
        check_vma=False,
    )
```

```python
import jax
import jax.numpy as jnp
from jax import lax
from jax.sharding import PartitionSpec as P

ITERS = 3


unobserved_weight = 25.0
ridge = 0.1


def exchange(values):
    return lax.all_to_all(values, ("rows", "grp"), 0, 0, tiled=True)


def sum_over_devices(value):
    for axis in ("grp", "rows"):
        size = lax.axis_size(axis)
        stride = 1
        while stride < size:
            partners = [(i, i ^ stride) for i in range(size)]
            value = value + lax.ppermute(value, axis, partners)
            stride *= 2
    return value


def on_device(item_table, histories, counts):
    row_count = lax.axis_size("rows")
    group_count = lax.axis_size("grp")
    devices = row_count * group_count
    table_rows, embed_width = item_table.shape
    user_count, history_length = histories.shape
    lookups = user_count * history_length
    capacity = max(4, 2 * lookups // devices)
    slots_total = devices * capacity
    bf16 = jnp.bfloat16
    f32 = jnp.float32

    local_gram = lax.dot_general(
        item_table, item_table, (((0,), (0,)), ((), ())), preferred_element_type=f32
    )
    gramian = sum_over_devices(local_gram)

    positions = lax.broadcasted_iota(jnp.int32, (user_count, history_length), 1)
    live = positions < counts[:, None]
    owners = histories // table_rows
    local_rows = histories - owners * table_rows
    owner_ids = lax.broadcasted_iota(jnp.int32, (user_count, history_length, devices), 2)
    by_owner = ((owners[:, :, None] == owner_ids) & live[:, :, None]).astype(bf16)
    per_user = jnp.sum(by_owner.astype(f32), axis=1)
    user_ids = lax.broadcasted_iota(jnp.int32, (user_count, user_count), 0)
    earlier_users = (lax.broadcasted_iota(jnp.int32, (user_count, user_count), 1) < user_ids).astype(bf16)
    before_user = jnp.einsum("uv,vo->uo", earlier_users, per_user.astype(bf16), preferred_element_type=f32)
    companions = jnp.concatenate([by_owner, before_user.astype(bf16)[:, None, :]], axis=1)
    same = jnp.einsum("ujo,uko->ujk", by_owner, companions, preferred_element_type=f32)
    slot_ids = lax.broadcasted_iota(jnp.int32, (history_length, history_length + 1), 0)
    other_ids = lax.broadcasted_iota(jnp.int32, (history_length, history_length + 1), 1)
    counted = ((other_ids < slot_ids) | (other_ids == history_length)).astype(f32)
    ranks = jnp.sum(same * counted[None], axis=2).astype(jnp.int32).reshape(lookups)

    flat_rows = local_rows.reshape(lookups, 1)
    row_high = flat_rows // 32
    row_low = flat_rows - row_high * 32
    user_of = lax.broadcasted_iota(jnp.int32, (user_count, history_length), 0).reshape(lookups, 1)
    flat_live = live.reshape(lookups, 1)
    columns = lax.broadcasted_iota(jnp.int32, (lookups, 4 * capacity), 1)
    part = columns // capacity
    chosen = (columns - part * capacity == ranks[:, None]) & flat_live
    value = jnp.where(
        part == 0, row_high, jnp.where(part == 1, row_low, jnp.where(part == 2, user_of, 1))
    )
    spread = jnp.where(chosen, value, 0).astype(bf16)
    slots = jnp.einsum(
        "io,ic->oc", by_owner.reshape(lookups, devices), spread, preferred_element_type=f32
    ).reshape(devices, 4, capacity)
    slots = slots.astype(jnp.int32)
    requests = slots[:, 0] * 32 + slots[:, 1]
    slot_user = slots[:, 2].reshape(slots_total)
    slot_used = slots[:, 3].reshape(slots_total)

    slot_index = owners.reshape(lookups) * capacity + ranks

    incoming = exchange(requests).reshape(slots_total)
    table_ids = lax.broadcasted_iota(jnp.int32, (slots_total, table_rows), 1)
    picks = (incoming[:, None] == table_ids).astype(bf16)
    answered = jnp.dot(picks, item_table, preferred_element_type=f32).astype(bf16)
    reply_rows = exchange(answered.reshape(devices, capacity, embed_width)).reshape(
        slots_total, embed_width
    )
    fetched = jnp.take(reply_rows, slot_index, axis=0, mode="clip").reshape(
        user_count, history_length, embed_width
    )
    weights = live.astype(f32)
    narrow_weights = weights.astype(bf16)
    target = jnp.einsum("ul,ulk->uk", narrow_weights, fetched, preferred_element_type=f32)
    unseen_scale = unobserved_weight / (table_rows * devices)
    solution = jnp.zeros_like(target)
    residual = target
    direction = target
    norm_now = jnp.sum(residual * residual, axis=1)
    for iteration in range(ITERS):
        narrow = direction.astype(bf16)
        scores = jnp.einsum("ulk,uk->ul", fetched, narrow, preferred_element_type=f32)
        scores = (scores * weights).astype(bf16)
        returned = jnp.einsum("ulk,ul->uk", fetched, scores, preferred_element_type=f32)
        curved = jnp.dot(direction, gramian, precision=lax.Precision.HIGHEST)
        applied = unseen_scale * curved + returned + ridge * direction
        step_size = norm_now / jnp.sum(direction * applied, axis=1)
        solution = solution + step_size[:, None] * direction
        residual = residual - step_size[:, None] * applied
        norm_next = jnp.sum(residual * residual, axis=1)
        direction = residual + (norm_next / norm_now)[:, None] * direction
        norm_now = norm_next

    member_ids = lax.broadcasted_iota(jnp.int32, (slots_total, user_count), 1)
    member = ((slot_user[:, None] == member_ids) & (slot_used[:, None] > 0)).astype(bf16)
    partials = jnp.einsum("su,uk->sk", member, solution.astype(bf16), preferred_element_type=f32)
    partials = partials.astype(bf16).reshape(devices, capacity, embed_width)
    arrived = exchange(partials).reshape(slots_total, embed_width)
    item_rhs = jnp.einsum("st,sk->tk", picks, arrived, preferred_element_type=f32)
    return (solution, item_rhs)


def solution(mesh):
    return jax.shard_map(
        on_device,
        mesh=mesh,
        in_specs=(P(("rows", "grp"), None), P(("rows", "grp"), None), P(("rows", "grp"))),
        out_specs=(P(("rows", "grp"), None), P(("rows", "grp"), None)),
        check_vma=False,
    )
```

```python
import jax
import jax.numpy as jnp
from jax import lax
from jax.sharding import PartitionSpec as P

ITERS = 3


unobserved_weight = 25.0
ridge = 0.1


def exchange(values):
    return lax.all_to_all(values, ("rows", "grp"), 0, 0, tiled=True)


def sum_over_devices(value):
    for axis in ("grp", "rows"):
        size = lax.axis_size(axis)
        stride = 1
        while stride < size:
            partners = [(i, i ^ stride) for i in range(size)]
            value = value + lax.ppermute(value, axis, partners)
            stride *= 2
    return value


def on_device(item_table, histories, counts):
    row_count = lax.axis_size("rows")
    group_count = lax.axis_size("grp")
    devices = row_count * group_count
    table_rows, embed_width = item_table.shape
    user_count, history_length = histories.shape
    lookups = user_count * history_length
    capacity = max(4, 2 * lookups // devices)
    slots_total = devices * capacity
    bf16 = jnp.bfloat16
    f32 = jnp.float32

    local_gram = lax.dot_general(
        item_table, item_table, (((0,), (0,)), ((), ())), preferred_element_type=f32
    )
    gramian = sum_over_devices(local_gram)

    positions = lax.broadcasted_iota(jnp.int32, (user_count, history_length), 1)
    live = positions < counts[:, None]
    owners = histories // table_rows
    local_rows = histories - owners * table_rows
    owner_ids = lax.broadcasted_iota(jnp.int32, (user_count, history_length, devices), 2)
    by_owner = ((owners[:, :, None] == owner_ids) & live[:, :, None]).astype(bf16)
    per_user = jnp.sum(by_owner.astype(f32), axis=1)
    user_ids = lax.broadcasted_iota(jnp.int32, (user_count, user_count), 0)
    earlier_users = (lax.broadcasted_iota(jnp.int32, (user_count, user_count), 1) < user_ids).astype(bf16)
    before_user = jnp.einsum("uv,vo->uo", earlier_users, per_user.astype(bf16), preferred_element_type=f32)
    companions = jnp.concatenate([by_owner, before_user.astype(bf16)[:, None, :]], axis=1)
    same = jnp.einsum("ujo,uko->ujk", by_owner, companions, preferred_element_type=f32)
    slot_ids = lax.broadcasted_iota(jnp.int32, (history_length, history_length + 1), 0)
    other_ids = lax.broadcasted_iota(jnp.int32, (history_length, history_length + 1), 1)
    counted = ((other_ids < slot_ids) | (other_ids == history_length)).astype(f32)
    ranks = jnp.sum(same * counted[None], axis=2).astype(jnp.int32).reshape(lookups)

    flat_rows = local_rows.reshape(lookups, 1)
    row_high = flat_rows // 32
    row_low = flat_rows - row_high * 32
    user_of = lax.broadcasted_iota(jnp.int32, (user_count, history_length), 0).reshape(lookups, 1)
    flat_live = live.reshape(lookups, 1)
    columns = lax.broadcasted_iota(jnp.int32, (lookups, 4 * capacity), 1)
    part = columns // capacity
    chosen = (columns - part * capacity == ranks[:, None]) & flat_live
    value = jnp.where(
        part == 0, row_high, jnp.where(part == 1, row_low, jnp.where(part == 2, user_of, 1))
    )
    spread = jnp.where(chosen, value, 0).astype(bf16)
    slots = jnp.einsum(
        "io,ic->oc", by_owner.reshape(lookups, devices), spread, preferred_element_type=f32
    ).reshape(devices, 4, capacity)
    slots = slots.astype(jnp.int32)
    requests = slots[:, 0] * 32 + slots[:, 1]
    slot_user = slots[:, 2].reshape(slots_total)
    slot_used = slots[:, 3].reshape(slots_total)

    slot_index = owners.reshape(lookups) * capacity + ranks

    incoming = exchange(requests).reshape(slots_total)
    table_ids = lax.broadcasted_iota(jnp.int32, (slots_total, table_rows), 1)
    picks = (incoming[:, None] == table_ids).astype(bf16)
    answered = jnp.dot(picks, item_table, preferred_element_type=f32).astype(bf16)
    reply_rows = exchange(answered.reshape(devices, capacity, embed_width)).reshape(
        slots_total, embed_width
    )
    fetched = reply_rows.astype(f32).at[slot_index].get(mode="promise_in_bounds")
    fetched = fetched.astype(bf16).reshape(user_count, history_length, embed_width)
    weights = live.astype(f32)
    narrow_weights = weights.astype(bf16)
    target = jnp.einsum("ul,ulk->uk", narrow_weights, fetched, preferred_element_type=f32)
    unseen_scale = unobserved_weight / (table_rows * devices)
    solution = jnp.zeros_like(target)
    residual = target
    direction = target
    norm_now = jnp.sum(residual * residual, axis=1)
    for iteration in range(ITERS):
        narrow = direction.astype(bf16)
        scores = jnp.einsum("ulk,uk->ul", fetched, narrow, preferred_element_type=f32)
        scores = (scores * weights).astype(bf16)
        returned = jnp.einsum("ulk,ul->uk", fetched, scores, preferred_element_type=f32)
        curved = jnp.dot(direction, gramian, precision=lax.Precision.HIGHEST)
        applied = unseen_scale * curved + returned + ridge * direction
        step_size = norm_now / jnp.sum(direction * applied, axis=1)
        solution = solution + step_size[:, None] * direction
        residual = residual - step_size[:, None] * applied
        norm_next = jnp.sum(residual * residual, axis=1)
        direction = residual + (norm_next / norm_now)[:, None] * direction
        norm_now = norm_next

    member_ids = lax.broadcasted_iota(jnp.int32, (slots_total, user_count), 1)
    member = ((slot_user[:, None] == member_ids) & (slot_used[:, None] > 0)).astype(bf16)
    partials = jnp.einsum("su,uk->sk", member, solution.astype(bf16), preferred_element_type=f32)
    partials = partials.astype(bf16).reshape(devices, capacity, embed_width)
    arrived = exchange(partials).reshape(slots_total, embed_width)
    item_rhs = jnp.einsum("st,sk->tk", picks, arrived, preferred_element_type=f32)
    return (solution, item_rhs)


def solution(mesh):
    return jax.shard_map(
        on_device,
        mesh=mesh,
        in_specs=(P(("rows", "grp"), None), P(("rows", "grp"), None), P(("rows", "grp"))),
        out_specs=(P(("rows", "grp"), None), P(("rows", "grp"), None)),
        check_vma=False,
    )
```

```python
import jax
import jax.numpy as jnp
from jax import lax
from jax.experimental import pallas as pl
from jax.experimental.pallas import tpu as pltpu
from jax.sharding import PartitionSpec as P

ITERS = 3


unobserved_weight = 25.0
ridge = 0.1


def exchange(values):
    return lax.all_to_all(values, ("rows", "grp"), 0, 0, tiled=True)


def sum_over_devices(value):
    for axis in ("grp", "rows"):
        size = lax.axis_size(axis)
        stride = 1
        while stride < size:
            partners = [(i, i ^ stride) for i in range(size)]
            value = value + lax.ppermute(value, axis, partners)
            stride *= 2
    return value


def gather_rows_kernel(index_ref, source_ref, out_ref):
    def body(i, carry):
        out_ref[pl.ds(i, 1), :] = source_ref[pl.ds(index_ref[i], 1), :]
        return carry

    lax.fori_loop(0, out_ref.shape[0], body, 0, unroll=8)


def gather_rows(source, index):
    count = index.shape[0]
    rows, width = source.shape
    wide = source.astype(jnp.float32)
    picked = pl.pallas_call(
        gather_rows_kernel,
        grid_spec=pltpu.PrefetchScalarGridSpec(
            num_scalar_prefetch=1,
            grid=(1,),
            in_specs=[pl.BlockSpec((rows, width), lambda i, index_ref: (0, 0))],
            out_specs=pl.BlockSpec((count, width), lambda i, index_ref: (0, 0)),
        ),
        out_shape=jax.ShapeDtypeStruct((count, width), jnp.float32),
    )(index, wide)
    return picked.astype(source.dtype)


def on_device(item_table, histories, counts):
    row_count = lax.axis_size("rows")
    group_count = lax.axis_size("grp")
    devices = row_count * group_count
    table_rows, embed_width = item_table.shape
    user_count, history_length = histories.shape
    lookups = user_count * history_length
    capacity = max(4, 2 * lookups // devices)
    slots_total = devices * capacity
    bf16 = jnp.bfloat16
    f32 = jnp.float32

    local_gram = lax.dot_general(
        item_table, item_table, (((0,), (0,)), ((), ())), preferred_element_type=f32
    )
    gramian = sum_over_devices(local_gram)

    positions = lax.broadcasted_iota(jnp.int32, (user_count, history_length), 1)
    live = positions < counts[:, None]
    owners = histories // table_rows
    local_rows = histories - owners * table_rows
    owner_ids = lax.broadcasted_iota(jnp.int32, (user_count, history_length, devices), 2)
    by_owner = ((owners[:, :, None] == owner_ids) & live[:, :, None]).astype(bf16)
    per_user = jnp.sum(by_owner.astype(f32), axis=1)
    user_ids = lax.broadcasted_iota(jnp.int32, (user_count, user_count), 0)
    earlier_users = (lax.broadcasted_iota(jnp.int32, (user_count, user_count), 1) < user_ids).astype(bf16)
    before_user = jnp.einsum("uv,vo->uo", earlier_users, per_user.astype(bf16), preferred_element_type=f32)
    companions = jnp.concatenate([by_owner, before_user.astype(bf16)[:, None, :]], axis=1)
    same = jnp.einsum("ujo,uko->ujk", by_owner, companions, preferred_element_type=f32)
    slot_ids = lax.broadcasted_iota(jnp.int32, (history_length, history_length + 1), 0)
    other_ids = lax.broadcasted_iota(jnp.int32, (history_length, history_length + 1), 1)
    counted = ((other_ids < slot_ids) | (other_ids == history_length)).astype(f32)
    ranks = jnp.sum(same * counted[None], axis=2).astype(jnp.int32).reshape(lookups)

    flat_rows = local_rows.reshape(lookups, 1)
    row_high = flat_rows // 32
    row_low = flat_rows - row_high * 32
    user_of = lax.broadcasted_iota(jnp.int32, (user_count, history_length), 0).reshape(lookups, 1)
    flat_live = live.reshape(lookups, 1)
    columns = lax.broadcasted_iota(jnp.int32, (lookups, 4 * capacity), 1)
    part = columns // capacity
    chosen = (columns - part * capacity == ranks[:, None]) & flat_live
    value = jnp.where(
        part == 0, row_high, jnp.where(part == 1, row_low, jnp.where(part == 2, user_of, 1))
    )
    spread = jnp.where(chosen, value, 0).astype(bf16)
    slots = jnp.einsum(
        "io,ic->oc", by_owner.reshape(lookups, devices), spread, preferred_element_type=f32
    ).reshape(devices, 4, capacity)
    slots = slots.astype(jnp.int32)
    requests = slots[:, 0] * 32 + slots[:, 1]
    slot_user = slots[:, 2].reshape(slots_total)
    slot_used = slots[:, 3].reshape(slots_total)

    slot_index = owners.reshape(lookups) * capacity + ranks

    incoming = exchange(requests).reshape(slots_total)
    table_ids = lax.broadcasted_iota(jnp.int32, (slots_total, table_rows), 1)
    picks = (incoming[:, None] == table_ids).astype(bf16)
    answered = jnp.dot(picks, item_table, preferred_element_type=f32).astype(bf16)
    reply_rows = exchange(answered.reshape(devices, capacity, embed_width)).reshape(
        slots_total, embed_width
    )
    fetched = gather_rows(reply_rows, slot_index).reshape(user_count, history_length, embed_width)
    weights = live.astype(f32)
    narrow_weights = weights.astype(bf16)
    target = jnp.einsum("ul,ulk->uk", narrow_weights, fetched, preferred_element_type=f32)
    unseen_scale = unobserved_weight / (table_rows * devices)
    solution = jnp.zeros_like(target)
    residual = target
    direction = target
    norm_now = jnp.sum(residual * residual, axis=1)
    for iteration in range(ITERS):
        narrow = direction.astype(bf16)
        scores = jnp.einsum("ulk,uk->ul", fetched, narrow, preferred_element_type=f32)
        scores = (scores * weights).astype(bf16)
        returned = jnp.einsum("ulk,ul->uk", fetched, scores, preferred_element_type=f32)
        curved = jnp.dot(direction, gramian, precision=lax.Precision.HIGHEST)
        applied = unseen_scale * curved + returned + ridge * direction
        step_size = norm_now / jnp.sum(direction * applied, axis=1)
        solution = solution + step_size[:, None] * direction
        residual = residual - step_size[:, None] * applied
        norm_next = jnp.sum(residual * residual, axis=1)
        direction = residual + (norm_next / norm_now)[:, None] * direction
        norm_now = norm_next

    member_ids = lax.broadcasted_iota(jnp.int32, (slots_total, user_count), 1)
    member = ((slot_user[:, None] == member_ids) & (slot_used[:, None] > 0)).astype(bf16)
    partials = jnp.einsum("su,uk->sk", member, solution.astype(bf16), preferred_element_type=f32)
    partials = partials.astype(bf16).reshape(devices, capacity, embed_width)
    arrived = exchange(partials).reshape(slots_total, embed_width)
    item_rhs = jnp.einsum("st,sk->tk", picks, arrived, preferred_element_type=f32)
    return (solution, item_rhs)


def solution(mesh):
    return jax.shard_map(
        on_device,
        mesh=mesh,
        in_specs=(P(("rows", "grp"), None), P(("rows", "grp"), None), P(("rows", "grp"))),
        out_specs=(P(("rows", "grp"), None), P(("rows", "grp"), None)),
        check_vma=False,
    )
```

```python
import jax
import jax.numpy as jnp
from jax import lax
from jax.experimental import pallas as pl
from jax.experimental.pallas import tpu as pltpu
from jax.sharding import PartitionSpec as P

ITERS = 3


unobserved_weight = 25.0
ridge = 0.1


def exchange(values):
    return lax.all_to_all(values, ("rows", "grp"), 0, 0, tiled=True)


def sum_over_devices(value):
    for axis in ("grp", "rows"):
        size = lax.axis_size(axis)
        stride = 1
        while stride < size:
            partners = [(i, i ^ stride) for i in range(size)]
            value = value + lax.ppermute(value, axis, partners)
            stride *= 2
    return value


def gather_rows_kernel(index_ref, source_ref, out_ref):
    def body(tile, carry):
        first = pl.multiple_of(tile * 8, 8)
        rows = [source_ref[pl.ds(index_ref[first + r], 1), :] for r in range(8)]
        out_ref[pl.ds(first, 8), :] = jnp.concatenate(rows, axis=0)
        return carry

    lax.fori_loop(0, out_ref.shape[0] // 8, body, 0, unroll=2)


def gather_rows(source, index):
    count = index.shape[0]
    rows, width = source.shape
    wide = source.astype(jnp.float32)
    picked = pl.pallas_call(
        gather_rows_kernel,
        grid_spec=pltpu.PrefetchScalarGridSpec(
            num_scalar_prefetch=1,
            grid=(1,),
            in_specs=[pl.BlockSpec((rows, width), lambda i, index_ref: (0, 0))],
            out_specs=pl.BlockSpec((count, width), lambda i, index_ref: (0, 0)),
        ),
        out_shape=jax.ShapeDtypeStruct((count, width), jnp.float32),
    )(index, wide)
    return picked.astype(source.dtype)


def on_device(item_table, histories, counts):
    row_count = lax.axis_size("rows")
    group_count = lax.axis_size("grp")
    devices = row_count * group_count
    table_rows, embed_width = item_table.shape
    user_count, history_length = histories.shape
    lookups = user_count * history_length
    capacity = max(4, 2 * lookups // devices)
    slots_total = devices * capacity
    bf16 = jnp.bfloat16
    f32 = jnp.float32

    local_gram = lax.dot_general(
        item_table, item_table, (((0,), (0,)), ((), ())), preferred_element_type=f32
    )
    gramian = sum_over_devices(local_gram)

    positions = lax.broadcasted_iota(jnp.int32, (user_count, history_length), 1)
    live = positions < counts[:, None]
    owners = histories // table_rows
    local_rows = histories - owners * table_rows
    owner_ids = lax.broadcasted_iota(jnp.int32, (user_count, history_length, devices), 2)
    by_owner = ((owners[:, :, None] == owner_ids) & live[:, :, None]).astype(bf16)
    per_user = jnp.sum(by_owner.astype(f32), axis=1)
    user_ids = lax.broadcasted_iota(jnp.int32, (user_count, user_count), 0)
    earlier_users = (lax.broadcasted_iota(jnp.int32, (user_count, user_count), 1) < user_ids).astype(bf16)
    before_user = jnp.einsum("uv,vo->uo", earlier_users, per_user.astype(bf16), preferred_element_type=f32)
    companions = jnp.concatenate([by_owner, before_user.astype(bf16)[:, None, :]], axis=1)
    same = jnp.einsum("ujo,uko->ujk", by_owner, companions, preferred_element_type=f32)
    slot_ids = lax.broadcasted_iota(jnp.int32, (history_length, history_length + 1), 0)
    other_ids = lax.broadcasted_iota(jnp.int32, (history_length, history_length + 1), 1)
    counted = ((other_ids < slot_ids) | (other_ids == history_length)).astype(f32)
    ranks = jnp.sum(same * counted[None], axis=2).astype(jnp.int32).reshape(lookups)

    flat_rows = local_rows.reshape(lookups, 1)
    row_high = flat_rows // 32
    row_low = flat_rows - row_high * 32
    user_of = lax.broadcasted_iota(jnp.int32, (user_count, history_length), 0).reshape(lookups, 1)
    flat_live = live.reshape(lookups, 1)
    columns = lax.broadcasted_iota(jnp.int32, (lookups, 4 * capacity), 1)
    part = columns // capacity
    chosen = (columns - part * capacity == ranks[:, None]) & flat_live
    value = jnp.where(
        part == 0, row_high, jnp.where(part == 1, row_low, jnp.where(part == 2, user_of, 1))
    )
    spread = jnp.where(chosen, value, 0).astype(bf16)
    slots = jnp.einsum(
        "io,ic->oc", by_owner.reshape(lookups, devices), spread, preferred_element_type=f32
    ).reshape(devices, 4, capacity)
    slots = slots.astype(jnp.int32)
    requests = slots[:, 0] * 32 + slots[:, 1]
    slot_user = slots[:, 2].reshape(slots_total)
    slot_used = slots[:, 3].reshape(slots_total)

    slot_index = owners.reshape(lookups) * capacity + ranks

    incoming = exchange(requests).reshape(slots_total)
    answered = gather_rows(item_table, incoming)
    reply_rows = exchange(answered.reshape(devices, capacity, embed_width)).reshape(
        slots_total, embed_width
    )
    fetched = gather_rows(reply_rows, slot_index).reshape(user_count, history_length, embed_width)
    weights = live.astype(f32)
    narrow_weights = weights.astype(bf16)
    target = jnp.einsum("ul,ulk->uk", narrow_weights, fetched, preferred_element_type=f32)
    unseen_scale = unobserved_weight / (table_rows * devices)
    solution = jnp.zeros_like(target)
    residual = target
    direction = target
    norm_now = jnp.sum(residual * residual, axis=1)
    for iteration in range(ITERS):
        narrow = direction.astype(bf16)
        scores = jnp.einsum("ulk,uk->ul", fetched, narrow, preferred_element_type=f32)
        scores = (scores * weights).astype(bf16)
        returned = jnp.einsum("ulk,ul->uk", fetched, scores, preferred_element_type=f32)
        curved = jnp.dot(direction, gramian, precision=lax.Precision.HIGHEST)
        applied = unseen_scale * curved + returned + ridge * direction
        step_size = norm_now / jnp.sum(direction * applied, axis=1)
        solution = solution + step_size[:, None] * direction
        residual = residual - step_size[:, None] * applied
        norm_next = jnp.sum(residual * residual, axis=1)
        direction = residual + (norm_next / norm_now)[:, None] * direction
        norm_now = norm_next

    member_ids = lax.broadcasted_iota(jnp.int32, (slots_total, user_count), 1)
    member = ((slot_user[:, None] == member_ids) & (slot_used[:, None] > 0)).astype(bf16)
    partials = jnp.einsum("su,uk->sk", member, solution.astype(bf16), preferred_element_type=f32)
    partials = partials.astype(bf16).reshape(devices, capacity, embed_width)
    arrived = exchange(partials).reshape(slots_total, embed_width)
    table_ids = lax.broadcasted_iota(jnp.int32, (slots_total, table_rows), 1)
    picks = (incoming[:, None] == table_ids).astype(bf16)
    item_rhs = jnp.einsum("st,sk->tk", picks, arrived, preferred_element_type=f32)
    return (solution, item_rhs)


def solution(mesh):
    return jax.shard_map(
        on_device,
        mesh=mesh,
        in_specs=(P(("rows", "grp"), None), P(("rows", "grp"), None), P(("rows", "grp"))),
        out_specs=(P(("rows", "grp"), None), P(("rows", "grp"), None)),
        check_vma=False,
    )
```

```python
import jax
import jax.numpy as jnp
from jax import lax
from jax.experimental import pallas as pl
from jax.experimental.pallas import tpu as pltpu
from jax.sharding import PartitionSpec as P

ITERS = 3


unobserved_weight = 25.0
ridge = 0.1


def exchange(values):
    return lax.all_to_all(values, ("rows", "grp"), 0, 0, tiled=True)


def sum_over_devices(value):
    for axis in ("grp", "rows"):
        size = lax.axis_size(axis)
        stride = 1
        while stride < size:
            partners = [(i, i ^ stride) for i in range(size)]
            value = value + lax.ppermute(value, axis, partners)
            stride *= 2
    return value


GATHER_TILE = 16


def gather_rows_kernel(index_ref, source_ref, out_ref):
    def body(tile, carry):
        first = pl.multiple_of(tile * GATHER_TILE, GATHER_TILE)
        rows = [source_ref[pl.ds(index_ref[first + r], 1), :] for r in range(GATHER_TILE)]
        out_ref[pl.ds(first, GATHER_TILE), :] = jnp.concatenate(rows, axis=0).astype(out_ref.dtype)
        return carry

    lax.fori_loop(0, out_ref.shape[0] // GATHER_TILE, body, 0)


def gather_rows(source, index):
    count = index.shape[0]
    rows, width = source.shape
    wide = source.astype(jnp.float32)
    picked = pl.pallas_call(
        gather_rows_kernel,
        grid_spec=pltpu.PrefetchScalarGridSpec(
            num_scalar_prefetch=1,
            grid=(1,),
            in_specs=[pl.BlockSpec((rows, width), lambda i, index_ref: (0, 0))],
            out_specs=pl.BlockSpec((count, width), lambda i, index_ref: (0, 0)),
        ),
        out_shape=jax.ShapeDtypeStruct((count, width), source.dtype),
    )(index, wide)
    return picked


def on_device(item_table, histories, counts):
    row_count = lax.axis_size("rows")
    group_count = lax.axis_size("grp")
    devices = row_count * group_count
    table_rows, embed_width = item_table.shape
    user_count, history_length = histories.shape
    lookups = user_count * history_length
    capacity = max(4, 2 * lookups // devices)
    slots_total = devices * capacity
    bf16 = jnp.bfloat16
    f32 = jnp.float32

    local_gram = lax.dot_general(
        item_table, item_table, (((0,), (0,)), ((), ())), preferred_element_type=f32
    )
    gramian = sum_over_devices(local_gram)

    positions = lax.broadcasted_iota(jnp.int32, (user_count, history_length), 1)
    live = positions < counts[:, None]
    owners = histories // table_rows
    local_rows = histories - owners * table_rows
    owner_ids = lax.broadcasted_iota(jnp.int32, (user_count, history_length, devices), 2)
    by_owner = ((owners[:, :, None] == owner_ids) & live[:, :, None]).astype(bf16)
    per_user = jnp.sum(by_owner.astype(f32), axis=1)
    user_ids = lax.broadcasted_iota(jnp.int32, (user_count, user_count), 0)
    earlier_users = (lax.broadcasted_iota(jnp.int32, (user_count, user_count), 1) < user_ids).astype(bf16)
    before_user = jnp.einsum("uv,vo->uo", earlier_users, per_user.astype(bf16), preferred_element_type=f32)
    companions = jnp.concatenate([by_owner, before_user.astype(bf16)[:, None, :]], axis=1)
    same = jnp.einsum("ujo,uko->ujk", by_owner, companions, preferred_element_type=f32)
    slot_ids = lax.broadcasted_iota(jnp.int32, (history_length, history_length + 1), 0)
    other_ids = lax.broadcasted_iota(jnp.int32, (history_length, history_length + 1), 1)
    counted = ((other_ids < slot_ids) | (other_ids == history_length)).astype(f32)
    ranks = jnp.sum(same * counted[None], axis=2).astype(jnp.int32).reshape(lookups)

    flat_rows = local_rows.reshape(lookups, 1)
    row_high = flat_rows // 32
    row_low = flat_rows - row_high * 32
    user_of = lax.broadcasted_iota(jnp.int32, (user_count, history_length), 0).reshape(lookups, 1)
    flat_live = live.reshape(lookups, 1)
    columns = lax.broadcasted_iota(jnp.int32, (lookups, 4 * capacity), 1)
    part = columns // capacity
    chosen = (columns - part * capacity == ranks[:, None]) & flat_live
    value = jnp.where(
        part == 0, row_high, jnp.where(part == 1, row_low, jnp.where(part == 2, user_of, 1))
    )
    spread = jnp.where(chosen, value, 0).astype(bf16)
    slots = jnp.einsum(
        "io,ic->oc", by_owner.reshape(lookups, devices), spread, preferred_element_type=f32
    ).reshape(devices, 4, capacity)
    slots = slots.astype(jnp.int32)
    requests = slots[:, 0] * 32 + slots[:, 1]
    slot_user = slots[:, 2].reshape(slots_total)
    slot_used = slots[:, 3].reshape(slots_total)

    slot_index = owners.reshape(lookups) * capacity + ranks

    incoming = exchange(requests).reshape(slots_total)
    answered = gather_rows(item_table, incoming)
    reply_rows = exchange(answered.reshape(devices, capacity, embed_width)).reshape(
        slots_total, embed_width
    )
    fetched = gather_rows(reply_rows, slot_index).reshape(user_count, history_length, embed_width)
    weights = live.astype(f32)
    narrow_weights = weights.astype(bf16)
    target = jnp.einsum("ul,ulk->uk", narrow_weights, fetched, preferred_element_type=f32)
    unseen_scale = unobserved_weight / (table_rows * devices)
    solution = jnp.zeros_like(target)
    residual = target
    direction = target
    norm_now = jnp.sum(residual * residual, axis=1)
    for iteration in range(ITERS):
        narrow = direction.astype(bf16)
        scores = jnp.einsum("ulk,uk->ul", fetched, narrow, preferred_element_type=f32)
        scores = (scores * weights).astype(bf16)
        returned = jnp.einsum("ulk,ul->uk", fetched, scores, preferred_element_type=f32)
        curved = jnp.dot(direction, gramian, precision=lax.Precision.HIGHEST)
        applied = unseen_scale * curved + returned + ridge * direction
        step_size = norm_now / jnp.sum(direction * applied, axis=1)
        solution = solution + step_size[:, None] * direction
        residual = residual - step_size[:, None] * applied
        norm_next = jnp.sum(residual * residual, axis=1)
        direction = residual + (norm_next / norm_now)[:, None] * direction
        norm_now = norm_next

    member_ids = lax.broadcasted_iota(jnp.int32, (slots_total, user_count), 1)
    member = ((slot_user[:, None] == member_ids) & (slot_used[:, None] > 0)).astype(bf16)
    partials = jnp.einsum("su,uk->sk", member, solution.astype(bf16), preferred_element_type=f32)
    partials = partials.astype(bf16).reshape(devices, capacity, embed_width)
    arrived = exchange(partials).reshape(slots_total, embed_width)
    table_ids = lax.broadcasted_iota(jnp.int32, (slots_total, table_rows), 1)
    picks = (incoming[:, None] == table_ids).astype(bf16)
    item_rhs = jnp.einsum("st,sk->tk", picks, arrived, preferred_element_type=f32)
    return (solution, item_rhs)


def solution(mesh):
    return jax.shard_map(
        on_device,
        mesh=mesh,
        in_specs=(P(("rows", "grp"), None), P(("rows", "grp"), None), P(("rows", "grp"))),
        out_specs=(P(("rows", "grp"), None), P(("rows", "grp"), None)),
        check_vma=False,
    )
```

```python
import jax
import jax.numpy as jnp
from jax import lax
from jax.experimental import pallas as pl
from jax.experimental.pallas import tpu as pltpu
from jax.sharding import PartitionSpec as P

ITERS = 3


unobserved_weight = 25.0
ridge = 0.1


def exchange(values):
    return lax.all_to_all(values, ("rows", "grp"), 0, 0, tiled=True)


def sum_over_devices(value):
    for axis in ("grp", "rows"):
        size = lax.axis_size(axis)
        stride = 1
        while stride < size:
            partners = [(i, i ^ stride) for i in range(size)]
            value = value + lax.ppermute(value, axis, partners)
            stride *= 2
    return value


GATHER_TILE = 16


def gather_rows_kernel(index_ref, source_ref, out_ref):
    def body(tile, carry):
        first = pl.multiple_of(tile * GATHER_TILE, GATHER_TILE)
        rows = [source_ref[pl.ds(index_ref[first + r], 1), :] for r in range(GATHER_TILE)]
        out_ref[pl.ds(first, GATHER_TILE), :] = jnp.concatenate(rows, axis=0).astype(out_ref.dtype)
        return carry

    lax.fori_loop(0, out_ref.shape[0] // GATHER_TILE, body, 0, unroll=4)


def gather_rows(source, index):
    count = index.shape[0]
    rows, width = source.shape
    wide = source.astype(jnp.float32)
    picked = pl.pallas_call(
        gather_rows_kernel,
        grid_spec=pltpu.PrefetchScalarGridSpec(
            num_scalar_prefetch=1,
            grid=(1,),
            in_specs=[pl.BlockSpec((rows, width), lambda i, index_ref: (0, 0))],
            out_specs=pl.BlockSpec((count, width), lambda i, index_ref: (0, 0)),
        ),
        out_shape=jax.ShapeDtypeStruct((count, width), source.dtype),
    )(index, wide)
    return picked


def on_device(item_table, histories, counts):
    row_count = lax.axis_size("rows")
    group_count = lax.axis_size("grp")
    devices = row_count * group_count
    table_rows, embed_width = item_table.shape
    user_count, history_length = histories.shape
    lookups = user_count * history_length
    capacity = max(4, 2 * lookups // devices)
    slots_total = devices * capacity
    bf16 = jnp.bfloat16
    f32 = jnp.float32

    local_gram = lax.dot_general(
        item_table, item_table, (((0,), (0,)), ((), ())), preferred_element_type=f32
    )
    gramian = sum_over_devices(local_gram)

    positions = lax.broadcasted_iota(jnp.int32, (user_count, history_length), 1)
    live = positions < counts[:, None]
    owners = histories // table_rows
    local_rows = histories - owners * table_rows
    owner_ids = lax.broadcasted_iota(jnp.int32, (user_count, history_length, devices), 2)
    by_owner = ((owners[:, :, None] == owner_ids) & live[:, :, None]).astype(bf16)
    per_user = jnp.sum(by_owner.astype(f32), axis=1)
    user_ids = lax.broadcasted_iota(jnp.int32, (user_count, user_count), 0)
    earlier_users = (lax.broadcasted_iota(jnp.int32, (user_count, user_count), 1) < user_ids).astype(bf16)
    before_user = jnp.einsum("uv,vo->uo", earlier_users, per_user.astype(bf16), preferred_element_type=f32)
    companions = jnp.concatenate([by_owner, before_user.astype(bf16)[:, None, :]], axis=1)
    same = jnp.einsum("ujo,uko->ujk", by_owner, companions, preferred_element_type=f32)
    slot_ids = lax.broadcasted_iota(jnp.int32, (history_length, history_length + 1), 0)
    other_ids = lax.broadcasted_iota(jnp.int32, (history_length, history_length + 1), 1)
    counted = ((other_ids < slot_ids) | (other_ids == history_length)).astype(f32)
    ranks = jnp.sum(same * counted[None], axis=2).astype(jnp.int32).reshape(lookups)

    flat_rows = local_rows.reshape(lookups, 1)
    row_high = flat_rows // 32
    row_low = flat_rows - row_high * 32
    user_of = lax.broadcasted_iota(jnp.int32, (user_count, history_length), 0).reshape(lookups, 1)
    flat_live = live.reshape(lookups, 1)
    columns = lax.broadcasted_iota(jnp.int32, (lookups, 4 * capacity), 1)
    part = columns // capacity
    chosen = (columns - part * capacity == ranks[:, None]) & flat_live
    value = jnp.where(
        part == 0, row_high, jnp.where(part == 1, row_low, jnp.where(part == 2, user_of, 1))
    )
    spread = jnp.where(chosen, value, 0).astype(bf16)
    slots = jnp.einsum(
        "io,ic->oc", by_owner.reshape(lookups, devices), spread, preferred_element_type=f32
    ).reshape(devices, 4, capacity)
    slots = slots.astype(jnp.int32)
    requests = slots[:, 0] * 32 + slots[:, 1]
    slot_user = slots[:, 2].reshape(slots_total)
    slot_used = slots[:, 3].reshape(slots_total)

    slot_index = owners.reshape(lookups) * capacity + ranks

    incoming = exchange(requests).reshape(slots_total)
    answered = gather_rows(item_table, incoming)
    reply_rows = exchange(answered.reshape(devices, capacity, embed_width)).reshape(
        slots_total, embed_width
    )
    fetched = gather_rows(reply_rows, slot_index).reshape(user_count, history_length, embed_width)
    weights = live.astype(f32)
    narrow_weights = weights.astype(bf16)
    target = jnp.einsum("ul,ulk->uk", narrow_weights, fetched, preferred_element_type=f32)
    unseen_scale = unobserved_weight / (table_rows * devices)
    solution = jnp.zeros_like(target)
    residual = target
    direction = target
    norm_now = jnp.sum(residual * residual, axis=1)
    for iteration in range(ITERS):
        narrow = direction.astype(bf16)
        scores = jnp.einsum("ulk,uk->ul", fetched, narrow, preferred_element_type=f32)
        scores = (scores * weights).astype(bf16)
        returned = jnp.einsum("ulk,ul->uk", fetched, scores, preferred_element_type=f32)
        curved = jnp.dot(direction, gramian, precision=lax.Precision.HIGHEST)
        applied = unseen_scale * curved + returned + ridge * direction
        step_size = norm_now / jnp.sum(direction * applied, axis=1)
        solution = solution + step_size[:, None] * direction
        residual = residual - step_size[:, None] * applied
        norm_next = jnp.sum(residual * residual, axis=1)
        direction = residual + (norm_next / norm_now)[:, None] * direction
        norm_now = norm_next

    member_ids = lax.broadcasted_iota(jnp.int32, (slots_total, user_count), 1)
    member = ((slot_user[:, None] == member_ids) & (slot_used[:, None] > 0)).astype(bf16)
    partials = jnp.einsum("su,uk->sk", member, solution.astype(bf16), preferred_element_type=f32)
    partials = partials.astype(bf16).reshape(devices, capacity, embed_width)
    arrived = exchange(partials).reshape(slots_total, embed_width)
    table_ids = lax.broadcasted_iota(jnp.int32, (slots_total, table_rows), 1)
    picks = (incoming[:, None] == table_ids).astype(bf16)
    item_rhs = jnp.einsum("st,sk->tk", picks, arrived, preferred_element_type=f32)
    return (solution, item_rhs)


def solution(mesh):
    return jax.shard_map(
        on_device,
        mesh=mesh,
        in_specs=(P(("rows", "grp"), None), P(("rows", "grp"), None), P(("rows", "grp"))),
        out_specs=(P(("rows", "grp"), None), P(("rows", "grp"), None)),
        check_vma=False,
    )
```

```python
import jax
import jax.numpy as jnp
from jax import lax
from jax.experimental import pallas as pl
from jax.experimental.pallas import tpu as pltpu
from jax.sharding import PartitionSpec as P

ITERS = 3


unobserved_weight = 25.0
ridge = 0.1


def exchange(values):
    return lax.all_to_all(values, ("rows", "grp"), 0, 0, tiled=True)


def sum_over_devices(value):
    for axis in ("grp", "rows"):
        size = lax.axis_size(axis)
        stride = 1
        while stride < size:
            partners = [(i, i ^ stride) for i in range(size)]
            value = value + lax.ppermute(value, axis, partners)
            stride *= 2
    return value


GATHER_TILE = 16


def gather_rows_kernel(index_ref, source_ref, out_ref):
    def body(tile, carry):
        first = pl.multiple_of(tile * GATHER_TILE, GATHER_TILE)
        rows = [source_ref[pl.ds(index_ref[first + r], 1), :] for r in range(GATHER_TILE)]
        out_ref[pl.ds(first, GATHER_TILE), :] = jnp.concatenate(rows, axis=0).astype(out_ref.dtype)
        return carry

    lax.fori_loop(0, out_ref.shape[0] // GATHER_TILE, body, 0, unroll=4)


def gather_rows(wide, index, dtype):
    count = index.shape[0]
    rows, width = wide.shape
    picked = pl.pallas_call(
        gather_rows_kernel,
        grid_spec=pltpu.PrefetchScalarGridSpec(
            num_scalar_prefetch=1,
            grid=(1,),
            in_specs=[pl.BlockSpec((rows, width), lambda i, index_ref: (0, 0))],
            out_specs=pl.BlockSpec((count, width), lambda i, index_ref: (0, 0)),
        ),
        out_shape=jax.ShapeDtypeStruct((count, width), dtype),
    )(index, wide)
    return picked


def on_device(item_table, histories, counts):
    row_count = lax.axis_size("rows")
    group_count = lax.axis_size("grp")
    devices = row_count * group_count
    table_rows, embed_width = item_table.shape
    user_count, history_length = histories.shape
    lookups = user_count * history_length
    capacity = max(4, 2 * lookups // devices)
    slots_total = devices * capacity
    bf16 = jnp.bfloat16
    f32 = jnp.float32

    local_gram = lax.dot_general(
        item_table, item_table, (((0,), (0,)), ((), ())), preferred_element_type=f32
    )

    positions = lax.broadcasted_iota(jnp.int32, (user_count, history_length), 1)
    live = positions < counts[:, None]
    owners = histories // table_rows
    local_rows = histories - owners * table_rows
    owner_ids = lax.broadcasted_iota(jnp.int32, (user_count, history_length, devices), 2)
    by_owner = ((owners[:, :, None] == owner_ids) & live[:, :, None]).astype(bf16)
    per_user = jnp.sum(by_owner.astype(f32), axis=1)
    user_ids = lax.broadcasted_iota(jnp.int32, (user_count, user_count), 0)
    earlier_users = (lax.broadcasted_iota(jnp.int32, (user_count, user_count), 1) < user_ids).astype(bf16)
    before_user = jnp.einsum("uv,vo->uo", earlier_users, per_user.astype(bf16), preferred_element_type=f32)
    companions = jnp.concatenate([by_owner, before_user.astype(bf16)[:, None, :]], axis=1)
    same = jnp.einsum("ujo,uko->ujk", by_owner, companions, preferred_element_type=f32)
    slot_ids = lax.broadcasted_iota(jnp.int32, (history_length, history_length + 1), 0)
    other_ids = lax.broadcasted_iota(jnp.int32, (history_length, history_length + 1), 1)
    counted = ((other_ids < slot_ids) | (other_ids == history_length)).astype(f32)
    ranks = jnp.sum(same * counted[None], axis=2).astype(jnp.int32).reshape(lookups)

    flat_rows = local_rows.reshape(lookups, 1)
    row_high = flat_rows // 32
    row_low = flat_rows - row_high * 32
    user_of = lax.broadcasted_iota(jnp.int32, (user_count, history_length), 0).reshape(lookups, 1)
    flat_live = live.reshape(lookups, 1)
    columns = lax.broadcasted_iota(jnp.int32, (lookups, 4 * capacity), 1)
    part = columns // capacity
    chosen = (columns - part * capacity == ranks[:, None]) & flat_live
    value = jnp.where(
        part == 0, row_high, jnp.where(part == 1, row_low, jnp.where(part == 2, user_of, 1))
    )
    spread = jnp.where(chosen, value, 0).astype(bf16)
    slots = jnp.einsum(
        "io,ic->oc", by_owner.reshape(lookups, devices), spread, preferred_element_type=f32
    ).reshape(devices, 4, capacity)
    slots = slots.astype(jnp.int32)
    requests = slots[:, 0] * 32 + slots[:, 1]
    slot_user = slots[:, 2].reshape(slots_total)
    slot_used = slots[:, 3].reshape(slots_total)


    gram_width = embed_width * embed_width // devices
    outgoing = jnp.concatenate(
        [requests.astype(f32), local_gram.reshape(devices, gram_width)], axis=1
    )
    received = exchange(outgoing)
    incoming = received[:, :capacity].astype(jnp.int32).reshape(slots_total)
    gram_slice = jnp.sum(received[:, capacity:], axis=0)
    high = lax.optimization_barrier(gram_slice.astype(bf16))
    rest = gram_slice - high.astype(f32)
    middle = lax.optimization_barrier(rest.astype(bf16))
    low = (rest - middle.astype(f32)).astype(bf16)
    pieces = jnp.concatenate([high, middle, low], axis=0)
    extra_rows = -(-pieces.shape[0] // embed_width)
    pieces = jnp.pad(pieces, (0, extra_rows * embed_width - pieces.shape[0]))
    source_rows = jnp.concatenate(
        [item_table.astype(f32), pieces.astype(f32).reshape(extra_rows, embed_width)], axis=0
    )
    reply_capacity = capacity + extra_rows
    piece_ids = jnp.broadcast_to(
        table_rows + jnp.arange(extra_rows, dtype=jnp.int32), (devices, extra_rows)
    )
    wanted = jnp.concatenate([incoming.reshape(devices, capacity), piece_ids], axis=1)
    answered = gather_rows(source_rows, wanted.reshape(devices * reply_capacity), bf16)
    replies = exchange(answered.reshape(devices, reply_capacity, embed_width))
    parts = replies[:, capacity:].reshape(devices, extra_rows * embed_width)[:, : 3 * gram_width]
    parts = parts.astype(f32).reshape(devices, 3, gram_width)
    gramian = ((parts[:, 0] + parts[:, 1]) + parts[:, 2]).reshape(embed_width, embed_width)
    reply_rows = replies.reshape(devices * reply_capacity, embed_width)
    slot_index = owners.reshape(lookups) * reply_capacity + ranks
    fetched = gather_rows(reply_rows.astype(f32), slot_index, bf16).reshape(
        user_count, history_length, embed_width
    )
    weights = live.astype(f32)
    narrow_weights = weights.astype(bf16)
    target = jnp.einsum("ul,ulk->uk", narrow_weights, fetched, preferred_element_type=f32)
    unseen_scale = unobserved_weight / (table_rows * devices)
    solution = jnp.zeros_like(target)
    residual = target
    direction = target
    norm_now = jnp.sum(residual * residual, axis=1)
    for iteration in range(ITERS):
        narrow = direction.astype(bf16)
        scores = jnp.einsum("ulk,uk->ul", fetched, narrow, preferred_element_type=f32)
        scores = (scores * weights).astype(bf16)
        returned = jnp.einsum("ulk,ul->uk", fetched, scores, preferred_element_type=f32)
        curved = jnp.dot(direction, gramian, precision=lax.Precision.HIGHEST)
        applied = unseen_scale * curved + returned + ridge * direction
        step_size = norm_now / jnp.sum(direction * applied, axis=1)
        solution = solution + step_size[:, None] * direction
        residual = residual - step_size[:, None] * applied
        norm_next = jnp.sum(residual * residual, axis=1)
        direction = residual + (norm_next / norm_now)[:, None] * direction
        norm_now = norm_next

    member_ids = lax.broadcasted_iota(jnp.int32, (slots_total, user_count), 1)
    member = ((slot_user[:, None] == member_ids) & (slot_used[:, None] > 0)).astype(bf16)
    partials = jnp.einsum("su,uk->sk", member, solution.astype(bf16), preferred_element_type=f32)
    partials = partials.astype(bf16).reshape(devices, capacity, embed_width)
    arrived = exchange(partials).reshape(slots_total, embed_width)
    table_ids = lax.broadcasted_iota(jnp.int32, (slots_total, table_rows), 1)
    picks = (incoming[:, None] == table_ids).astype(bf16)
    item_rhs = jnp.einsum("st,sk->tk", picks, arrived, preferred_element_type=f32)
    return (solution, item_rhs)


def solution(mesh):
    return jax.shard_map(
        on_device,
        mesh=mesh,
        in_specs=(P(("rows", "grp"), None), P(("rows", "grp"), None), P(("rows", "grp"))),
        out_specs=(P(("rows", "grp"), None), P(("rows", "grp"), None)),
        check_vma=False,
    )
```

```python
import jax
import jax.numpy as jnp
from jax import lax
from jax.experimental import pallas as pl
from jax.experimental.pallas import tpu as pltpu
from jax.sharding import PartitionSpec as P

ITERS = 3


unobserved_weight = 25.0
ridge = 0.1


def exchange(values):
    return lax.all_to_all(values, ("rows", "grp"), 0, 0, tiled=True)


def sum_over_devices(value):
    for axis in ("grp", "rows"):
        size = lax.axis_size(axis)
        stride = 1
        while stride < size:
            partners = [(i, i ^ stride) for i in range(size)]
            value = value + lax.ppermute(value, axis, partners)
            stride *= 2
    return value


GATHER_TILE = 16


def gather_rows_kernel(index_ref, source_ref, out_ref):
    def body(tile, carry):
        first = pl.multiple_of(tile * GATHER_TILE, GATHER_TILE)
        rows = [source_ref[pl.ds(index_ref[first + r], 1), :] for r in range(GATHER_TILE)]
        out_ref[pl.ds(first, GATHER_TILE), :] = jnp.concatenate(rows, axis=0).astype(out_ref.dtype)
        return carry

    lax.fori_loop(0, out_ref.shape[0] // GATHER_TILE, body, 0, unroll=4)


def gather_rows(wide, index, dtype):
    count = index.shape[0]
    rows, width = wide.shape
    picked = pl.pallas_call(
        gather_rows_kernel,
        grid_spec=pltpu.PrefetchScalarGridSpec(
            num_scalar_prefetch=1,
            grid=(1,),
            in_specs=[pl.BlockSpec((rows, width), lambda i, index_ref: (0, 0))],
            out_specs=pl.BlockSpec((count, width), lambda i, index_ref: (0, 0)),
        ),
        out_shape=jax.ShapeDtypeStruct((count, width), dtype),
    )(index, wide)
    return picked


def answer_kernel(index_ref, source_ref, out_ref):
    chunks, depth, _ = out_ref.shape
    capacity = index_ref.shape[0] // chunks
    table_rows = source_ref.shape[0] - (depth - capacity)
    extra = source_ref[pl.ds(table_rows, depth - capacity), :].astype(out_ref.dtype)

    def body(chunk, carry):
        for start in range(0, capacity, GATHER_TILE):
            first = chunk * capacity + start
            rows = [source_ref[pl.ds(index_ref[first + r], 1), :] for r in range(GATHER_TILE)]
            out_ref[chunk, pl.ds(start, GATHER_TILE), :] = jnp.concatenate(rows, axis=0).astype(
                out_ref.dtype
            )
        out_ref[chunk, pl.ds(capacity, depth - capacity), :] = extra
        return carry

    lax.fori_loop(0, chunks, body, 0, unroll=2)


def answer_rows(wide, index, chunks, depth, dtype):
    rows, width = wide.shape
    return pl.pallas_call(
        answer_kernel,
        grid_spec=pltpu.PrefetchScalarGridSpec(
            num_scalar_prefetch=1,
            grid=(1,),
            in_specs=[pl.BlockSpec((rows, width), lambda i, index_ref: (0, 0))],
            out_specs=pl.BlockSpec((chunks, depth, width), lambda i, index_ref: (0, 0, 0)),
        ),
        out_shape=jax.ShapeDtypeStruct((chunks, depth, width), dtype),
    )(index, wide)


def on_device(item_table, histories, counts):
    row_count = lax.axis_size("rows")
    group_count = lax.axis_size("grp")
    devices = row_count * group_count
    table_rows, embed_width = item_table.shape
    user_count, history_length = histories.shape
    lookups = user_count * history_length
    capacity = max(4, 2 * lookups // devices)
    slots_total = devices * capacity
    bf16 = jnp.bfloat16
    f32 = jnp.float32

    local_gram = lax.dot_general(
        item_table, item_table, (((0,), (0,)), ((), ())), preferred_element_type=f32
    )

    positions = lax.broadcasted_iota(jnp.int32, (user_count, history_length), 1)
    live = positions < counts[:, None]
    owners = histories // table_rows
    local_rows = histories - owners * table_rows
    owner_ids = lax.broadcasted_iota(jnp.int32, (user_count, history_length, devices), 2)
    by_owner = ((owners[:, :, None] == owner_ids) & live[:, :, None]).astype(bf16)
    per_user = jnp.sum(by_owner.astype(f32), axis=1)
    user_ids = lax.broadcasted_iota(jnp.int32, (user_count, user_count), 0)
    earlier_users = (lax.broadcasted_iota(jnp.int32, (user_count, user_count), 1) < user_ids).astype(bf16)
    before_user = jnp.einsum("uv,vo->uo", earlier_users, per_user.astype(bf16), preferred_element_type=f32)
    companions = jnp.concatenate([by_owner, before_user.astype(bf16)[:, None, :]], axis=1)
    same = jnp.einsum("ujo,uko->ujk", by_owner, companions, preferred_element_type=f32)
    slot_ids = lax.broadcasted_iota(jnp.int32, (history_length, history_length + 1), 0)
    other_ids = lax.broadcasted_iota(jnp.int32, (history_length, history_length + 1), 1)
    counted = ((other_ids < slot_ids) | (other_ids == history_length)).astype(f32)
    ranks = jnp.sum(same * counted[None], axis=2).astype(jnp.int32).reshape(lookups)

    flat_rows = local_rows.reshape(lookups, 1)
    row_high = flat_rows // 32
    row_low = flat_rows - row_high * 32
    user_of = lax.broadcasted_iota(jnp.int32, (user_count, history_length), 0).reshape(lookups, 1)
    flat_live = live.reshape(lookups, 1)
    columns = lax.broadcasted_iota(jnp.int32, (lookups, 4 * capacity), 1)
    part = columns // capacity
    chosen = (columns - part * capacity == ranks[:, None]) & flat_live
    value = jnp.where(
        part == 0, row_high, jnp.where(part == 1, row_low, jnp.where(part == 2, user_of, 1))
    )
    spread = jnp.where(chosen, value, 0).astype(bf16)
    slots = jnp.einsum(
        "io,ic->oc", by_owner.reshape(lookups, devices), spread, preferred_element_type=f32
    ).reshape(devices, 4, capacity)
    slots = slots.astype(jnp.int32)
    requests = slots[:, 0] * 32 + slots[:, 1]
    slot_user = slots[:, 2].reshape(slots_total)
    slot_used = slots[:, 3].reshape(slots_total)


    gram_width = embed_width * embed_width // devices
    outgoing = jnp.concatenate(
        [requests.astype(f32), local_gram.reshape(devices, gram_width)], axis=1
    )
    received = exchange(outgoing)
    incoming = received[:, :capacity].astype(jnp.int32).reshape(slots_total)
    gram_slice = jnp.sum(received[:, capacity:], axis=0)
    high = lax.optimization_barrier(gram_slice.astype(bf16))
    rest = gram_slice - high.astype(f32)
    middle = lax.optimization_barrier(rest.astype(bf16))
    low = (rest - middle.astype(f32)).astype(bf16)
    pieces = jnp.concatenate([high, middle, low], axis=0)
    extra_rows = -(-pieces.shape[0] // embed_width)
    pieces = jnp.pad(pieces, (0, extra_rows * embed_width - pieces.shape[0]))
    source_rows = jnp.concatenate(
        [item_table.astype(f32), pieces.astype(f32).reshape(extra_rows, embed_width)], axis=0
    )
    reply_capacity = capacity + extra_rows
    answered = answer_rows(source_rows, incoming, devices, reply_capacity, bf16)
    replies = exchange(answered)
    parts = replies[:, capacity:].reshape(devices, extra_rows * embed_width)[:, : 3 * gram_width]
    parts = parts.astype(f32).reshape(devices, 3, gram_width)
    gramian = ((parts[:, 0] + parts[:, 1]) + parts[:, 2]).reshape(embed_width, embed_width)
    reply_rows = replies.reshape(devices * reply_capacity, embed_width)
    slot_index = owners.reshape(lookups) * reply_capacity + ranks
    fetched = gather_rows(reply_rows.astype(f32), slot_index, bf16).reshape(
        user_count, history_length, embed_width
    )
    weights = live.astype(f32)
    narrow_weights = weights.astype(bf16)
    target = jnp.einsum("ul,ulk->uk", narrow_weights, fetched, preferred_element_type=f32)
    unseen_scale = unobserved_weight / (table_rows * devices)
    solution = jnp.zeros_like(target)
    residual = target
    direction = target
    norm_now = jnp.sum(residual * residual, axis=1)
    for iteration in range(ITERS):
        narrow = direction.astype(bf16)
        scores = jnp.einsum("ulk,uk->ul", fetched, narrow, preferred_element_type=f32)
        scores = (scores * weights).astype(bf16)
        returned = jnp.einsum("ulk,ul->uk", fetched, scores, preferred_element_type=f32)
        curved = jnp.dot(direction, gramian, precision=lax.Precision.HIGHEST)
        applied = unseen_scale * curved + returned + ridge * direction
        step_size = norm_now / jnp.sum(direction * applied, axis=1)
        solution = solution + step_size[:, None] * direction
        residual = residual - step_size[:, None] * applied
        norm_next = jnp.sum(residual * residual, axis=1)
        direction = residual + (norm_next / norm_now)[:, None] * direction
        norm_now = norm_next

    member_ids = lax.broadcasted_iota(jnp.int32, (slots_total, user_count), 1)
    member = ((slot_user[:, None] == member_ids) & (slot_used[:, None] > 0)).astype(bf16)
    partials = jnp.einsum("su,uk->sk", member, solution.astype(bf16), preferred_element_type=f32)
    partials = partials.astype(bf16).reshape(devices, capacity, embed_width)
    arrived = exchange(partials).reshape(slots_total, embed_width)
    table_ids = lax.broadcasted_iota(jnp.int32, (slots_total, table_rows), 1)
    picks = (incoming[:, None] == table_ids).astype(bf16)
    item_rhs = jnp.einsum("st,sk->tk", picks, arrived, preferred_element_type=f32)
    return (solution, item_rhs)


def solution(mesh):
    return jax.shard_map(
        on_device,
        mesh=mesh,
        in_specs=(P(("rows", "grp"), None), P(("rows", "grp"), None), P(("rows", "grp"))),
        out_specs=(P(("rows", "grp"), None), P(("rows", "grp"), None)),
        check_vma=False,
    )
```

```python
import jax
import jax.numpy as jnp
from jax import lax
from jax.experimental import pallas as pl
from jax.experimental.pallas import tpu as pltpu
from jax.sharding import PartitionSpec as P

ITERS = 3


unobserved_weight = 25.0
ridge = 0.1


def exchange(values):
    return lax.all_to_all(values, ("rows", "grp"), 0, 0, tiled=True)


def sum_over_devices(value):
    for axis in ("grp", "rows"):
        size = lax.axis_size(axis)
        stride = 1
        while stride < size:
            partners = [(i, i ^ stride) for i in range(size)]
            value = value + lax.ppermute(value, axis, partners)
            stride *= 2
    return value


GATHER_TILE = 16


def gather_rows_kernel(index_ref, source_ref, out_ref):
    def body(tile, carry):
        first = pl.multiple_of(tile * GATHER_TILE, GATHER_TILE)
        rows = [source_ref[pl.ds(index_ref[first + r], 1), :] for r in range(GATHER_TILE)]
        out_ref[pl.ds(first, GATHER_TILE), :] = jnp.concatenate(rows, axis=0).astype(out_ref.dtype)
        return carry

    lax.fori_loop(0, out_ref.shape[0] // GATHER_TILE, body, 0, unroll=8)


def gather_rows(wide, index, dtype):
    count = index.shape[0]
    rows, width = wide.shape
    picked = pl.pallas_call(
        gather_rows_kernel,
        grid_spec=pltpu.PrefetchScalarGridSpec(
            num_scalar_prefetch=1,
            grid=(1,),
            in_specs=[pl.BlockSpec((rows, width), lambda i, index_ref: (0, 0))],
            out_specs=pl.BlockSpec((count, width), lambda i, index_ref: (0, 0)),
        ),
        out_shape=jax.ShapeDtypeStruct((count, width), dtype),
    )(index, wide)
    return picked


def answer_kernel(index_ref, source_ref, out_ref):
    chunks, depth, _ = out_ref.shape
    capacity = index_ref.shape[0] // chunks
    table_rows = source_ref.shape[0] - (depth - capacity)
    extra = source_ref[pl.ds(table_rows, depth - capacity), :].astype(out_ref.dtype)

    def body(chunk, carry):
        for start in range(0, capacity, GATHER_TILE):
            first = chunk * capacity + start
            rows = [source_ref[pl.ds(index_ref[first + r], 1), :] for r in range(GATHER_TILE)]
            out_ref[chunk, pl.ds(start, GATHER_TILE), :] = jnp.concatenate(rows, axis=0).astype(
                out_ref.dtype
            )
        out_ref[chunk, pl.ds(capacity, depth - capacity), :] = extra
        return carry

    lax.fori_loop(0, chunks, body, 0, unroll=4)


def answer_rows(wide, index, chunks, depth, dtype):
    rows, width = wide.shape
    return pl.pallas_call(
        answer_kernel,
        grid_spec=pltpu.PrefetchScalarGridSpec(
            num_scalar_prefetch=1,
            grid=(1,),
            in_specs=[pl.BlockSpec((rows, width), lambda i, index_ref: (0, 0))],
            out_specs=pl.BlockSpec((chunks, depth, width), lambda i, index_ref: (0, 0, 0)),
        ),
        out_shape=jax.ShapeDtypeStruct((chunks, depth, width), dtype),
    )(index, wide)


def on_device(item_table, histories, counts):
    row_count = lax.axis_size("rows")
    group_count = lax.axis_size("grp")
    devices = row_count * group_count
    table_rows, embed_width = item_table.shape
    user_count, history_length = histories.shape
    lookups = user_count * history_length
    capacity = max(4, 2 * lookups // devices)
    slots_total = devices * capacity
    bf16 = jnp.bfloat16
    f32 = jnp.float32

    local_gram = lax.dot_general(
        item_table, item_table, (((0,), (0,)), ((), ())), preferred_element_type=f32
    )

    positions = lax.broadcasted_iota(jnp.int32, (user_count, history_length), 1)
    live = positions < counts[:, None]
    owners = histories // table_rows
    local_rows = histories - owners * table_rows
    owner_ids = lax.broadcasted_iota(jnp.int32, (user_count, history_length, devices), 2)
    by_owner = ((owners[:, :, None] == owner_ids) & live[:, :, None]).astype(bf16)
    per_user = jnp.sum(by_owner.astype(f32), axis=1)
    user_ids = lax.broadcasted_iota(jnp.int32, (user_count, user_count), 0)
    earlier_users = (lax.broadcasted_iota(jnp.int32, (user_count, user_count), 1) < user_ids).astype(bf16)
    before_user = jnp.einsum("uv,vo->uo", earlier_users, per_user.astype(bf16), preferred_element_type=f32)
    companions = jnp.concatenate([by_owner, before_user.astype(bf16)[:, None, :]], axis=1)
    same = jnp.einsum("ujo,uko->ujk", by_owner, companions, preferred_element_type=f32)
    slot_ids = lax.broadcasted_iota(jnp.int32, (history_length, history_length + 1), 0)
    other_ids = lax.broadcasted_iota(jnp.int32, (history_length, history_length + 1), 1)
    counted = ((other_ids < slot_ids) | (other_ids == history_length)).astype(f32)
    ranks = jnp.einsum("ujk,jk->uj", same, counted).astype(jnp.int32).reshape(lookups)

    flat_rows = local_rows.reshape(lookups, 1)
    row_high = flat_rows // 32
    row_low = flat_rows - row_high * 32
    user_of = lax.broadcasted_iota(jnp.int32, (user_count, history_length), 0).reshape(lookups, 1)
    flat_live = live.reshape(lookups, 1)
    columns = lax.broadcasted_iota(jnp.int32, (lookups, 4 * capacity), 1)
    part = columns // capacity
    chosen = (columns - part * capacity == ranks[:, None]) & flat_live
    value = jnp.where(
        part == 0, row_high, jnp.where(part == 1, row_low, jnp.where(part == 2, user_of, 1))
    )
    spread = jnp.where(chosen, value, 0).astype(bf16)
    slots = jnp.einsum(
        "io,ic->oc", by_owner.reshape(lookups, devices), spread, preferred_element_type=f32
    ).reshape(devices, 4, capacity)
    slots = slots.astype(jnp.int32)
    requests = slots[:, 0] * 32 + slots[:, 1]
    slot_user = slots[:, 2].reshape(slots_total)
    slot_used = slots[:, 3].reshape(slots_total)


    gram_width = embed_width * embed_width // devices
    outgoing = jnp.concatenate(
        [requests.astype(f32), local_gram.reshape(devices, gram_width)], axis=1
    )
    received = exchange(outgoing)
    incoming = received[:, :capacity].astype(jnp.int32).reshape(slots_total)
    gram_slice = jnp.sum(received[:, capacity:], axis=0)
    high = lax.optimization_barrier(gram_slice.astype(bf16))
    rest = gram_slice - high.astype(f32)
    middle = lax.optimization_barrier(rest.astype(bf16))
    low = (rest - middle.astype(f32)).astype(bf16)
    pieces = jnp.concatenate([high, middle, low], axis=0)
    extra_rows = -(-pieces.shape[0] // embed_width)
    pieces = jnp.pad(pieces, (0, extra_rows * embed_width - pieces.shape[0]))
    source_rows = jnp.concatenate(
        [item_table.astype(f32), pieces.astype(f32).reshape(extra_rows, embed_width)], axis=0
    )
    reply_capacity = capacity + extra_rows
    answered = answer_rows(source_rows, incoming, devices, reply_capacity, bf16)
    replies = exchange(answered)
    parts = replies[:, capacity:].reshape(devices, extra_rows * embed_width)[:, : 3 * gram_width]
    parts = parts.astype(f32).reshape(devices, 3, gram_width)
    gramian = ((parts[:, 0] + parts[:, 1]) + parts[:, 2]).reshape(embed_width, embed_width)
    reply_rows = replies.reshape(devices * reply_capacity, embed_width)
    slot_index = owners.reshape(lookups) * reply_capacity + ranks
    fetched = gather_rows(reply_rows.astype(f32), slot_index, bf16).reshape(
        user_count, history_length, embed_width
    )
    weights = live.astype(f32)
    narrow_weights = weights.astype(bf16)
    target = jnp.einsum("ul,ulk->uk", narrow_weights, fetched, preferred_element_type=f32)
    unseen_scale = unobserved_weight / (table_rows * devices)
    solution = jnp.zeros_like(target)
    residual = target
    direction = target
    norm_now = jnp.sum(residual * residual, axis=1)
    for iteration in range(ITERS):
        narrow = direction.astype(bf16)
        scores = jnp.einsum("ulk,uk->ul", fetched, narrow, preferred_element_type=f32)
        scores = (scores * weights).astype(bf16)
        returned = jnp.einsum("ulk,ul->uk", fetched, scores, preferred_element_type=f32)
        curved = jnp.dot(direction, gramian, precision=lax.Precision.HIGHEST)
        applied = unseen_scale * curved + returned + ridge * direction
        step_size = norm_now / jnp.sum(direction * applied, axis=1)
        solution = solution + step_size[:, None] * direction
        residual = residual - step_size[:, None] * applied
        norm_next = jnp.sum(residual * residual, axis=1)
        direction = residual + (norm_next / norm_now)[:, None] * direction
        norm_now = norm_next

    member_ids = lax.broadcasted_iota(jnp.int32, (slots_total, user_count), 1)
    member = ((slot_user[:, None] == member_ids) & (slot_used[:, None] > 0)).astype(bf16)
    partials = jnp.einsum("su,uk->sk", member, solution.astype(bf16), preferred_element_type=f32)
    partials = partials.astype(bf16).reshape(devices, capacity, embed_width)
    arrived = exchange(partials).reshape(slots_total, embed_width)
    table_ids = lax.broadcasted_iota(jnp.int32, (slots_total, table_rows), 1)
    picks = (incoming[:, None] == table_ids).astype(bf16)
    item_rhs = jnp.einsum("st,sk->tk", picks, arrived, preferred_element_type=f32)
    return (solution, item_rhs)


def solution(mesh):
    return jax.shard_map(
        on_device,
        mesh=mesh,
        in_specs=(P(("rows", "grp"), None), P(("rows", "grp"), None), P(("rows", "grp"))),
        out_specs=(P(("rows", "grp"), None), P(("rows", "grp"), None)),
        check_vma=False,
    )
```

```python
import jax
import jax.numpy as jnp
from jax import lax
from jax.experimental import pallas as pl
from jax.experimental.pallas import tpu as pltpu
from jax.sharding import PartitionSpec as P

ITERS = 3


unobserved_weight = 25.0
ridge = 0.1


def exchange(values):
    return lax.all_to_all(values, ("rows", "grp"), 0, 0, tiled=True)


def sum_over_devices(value):
    for axis in ("grp", "rows"):
        size = lax.axis_size(axis)
        stride = 1
        while stride < size:
            partners = [(i, i ^ stride) for i in range(size)]
            value = value + lax.ppermute(value, axis, partners)
            stride *= 2
    return value


GATHER_TILE = 16


def gather_rows_kernel(index_ref, source_ref, out_ref):
    def body(tile, carry):
        first = pl.multiple_of(tile * GATHER_TILE, GATHER_TILE)
        rows = [source_ref[pl.ds(index_ref[first + r], 1), :] for r in range(GATHER_TILE)]
        out_ref[pl.ds(first, GATHER_TILE), :] = jnp.concatenate(rows, axis=0).astype(out_ref.dtype)
        return carry

    lax.fori_loop(0, out_ref.shape[0] // GATHER_TILE, body, 0, unroll=8)


def gather_rows(wide, index, dtype):
    count = index.shape[0]
    rows, width = wide.shape
    picked = pl.pallas_call(
        gather_rows_kernel,
        grid_spec=pltpu.PrefetchScalarGridSpec(
            num_scalar_prefetch=1,
            grid=(1,),
            in_specs=[pl.BlockSpec((rows, width), lambda i, index_ref: (0, 0))],
            out_specs=pl.BlockSpec((count, width), lambda i, index_ref: (0, 0)),
        ),
        out_shape=jax.ShapeDtypeStruct((count, width), dtype),
    )(index, wide)
    return picked


def answer_kernel(index_ref, source_ref, out_ref):
    chunks, depth, _ = out_ref.shape
    capacity = index_ref.shape[0] // chunks
    table_rows = source_ref.shape[0] - (depth - capacity)
    extra = source_ref[pl.ds(table_rows, depth - capacity), :].astype(out_ref.dtype)

    def body(chunk, carry):
        for start in range(0, capacity, GATHER_TILE):
            first = chunk * capacity + start
            rows = [source_ref[pl.ds(index_ref[first + r], 1), :] for r in range(GATHER_TILE)]
            out_ref[chunk, pl.ds(start, GATHER_TILE), :] = jnp.concatenate(rows, axis=0).astype(
                out_ref.dtype
            )
        out_ref[chunk, pl.ds(capacity, depth - capacity), :] = extra
        return carry

    lax.fori_loop(0, chunks, body, 0, unroll=4)


def answer_rows(wide, index, chunks, depth, dtype):
    rows, width = wide.shape
    return pl.pallas_call(
        answer_kernel,
        grid_spec=pltpu.PrefetchScalarGridSpec(
            num_scalar_prefetch=1,
            grid=(1,),
            in_specs=[pl.BlockSpec((rows, width), lambda i, index_ref: (0, 0))],
            out_specs=pl.BlockSpec((chunks, depth, width), lambda i, index_ref: (0, 0, 0)),
        ),
        out_shape=jax.ShapeDtypeStruct((chunks, depth, width), dtype),
    )(index, wide)


def fetch_kernel(owner_ref, rank_ref, source_ref, out_ref, wide_ref):
    wide_ref[...] = source_ref[...].astype(jnp.float32)

    def body(tile, carry):
        first = pl.multiple_of(tile * GATHER_TILE, GATHER_TILE)
        rows = [
            wide_ref[owner_ref[first + r], pl.ds(rank_ref[first + r], 1), :]
            for r in range(GATHER_TILE)
        ]
        out_ref[pl.ds(first, GATHER_TILE), :] = jnp.concatenate(rows, axis=0).astype(out_ref.dtype)
        return carry

    lax.fori_loop(0, out_ref.shape[0] // GATHER_TILE, body, 0, unroll=8)


def fetch_rows(source, owner, rank):
    count = owner.shape[0]
    return pl.pallas_call(
        fetch_kernel,
        grid_spec=pltpu.PrefetchScalarGridSpec(
            num_scalar_prefetch=2,
            grid=(1,),
            in_specs=[pl.BlockSpec(source.shape, lambda i, owner_ref, rank_ref: (0, 0, 0))],
            out_specs=pl.BlockSpec((count, source.shape[2]), lambda i, owner_ref, rank_ref: (0, 0)),
            scratch_shapes=[pltpu.VMEM(source.shape, jnp.float32)],
        ),
        out_shape=jax.ShapeDtypeStruct((count, source.shape[2]), source.dtype),
    )(owner, rank, source)


def on_device(item_table, histories, counts):
    row_count = lax.axis_size("rows")
    group_count = lax.axis_size("grp")
    devices = row_count * group_count
    table_rows, embed_width = item_table.shape
    user_count, history_length = histories.shape
    lookups = user_count * history_length
    capacity = max(4, 2 * lookups // devices)
    slots_total = devices * capacity
    bf16 = jnp.bfloat16
    f32 = jnp.float32

    local_gram = lax.dot_general(
        item_table, item_table, (((0,), (0,)), ((), ())), preferred_element_type=f32
    )

    positions = lax.broadcasted_iota(jnp.int32, (user_count, history_length), 1)
    live = positions < counts[:, None]
    owners = histories // table_rows
    local_rows = histories - owners * table_rows
    owner_ids = lax.broadcasted_iota(jnp.int32, (user_count, history_length, devices), 2)
    by_owner = ((owners[:, :, None] == owner_ids) & live[:, :, None]).astype(bf16)
    per_user = jnp.sum(by_owner.astype(f32), axis=1)
    user_ids = lax.broadcasted_iota(jnp.int32, (user_count, user_count), 0)
    earlier_users = (lax.broadcasted_iota(jnp.int32, (user_count, user_count), 1) < user_ids).astype(bf16)
    before_user = jnp.einsum("uv,vo->uo", earlier_users, per_user.astype(bf16), preferred_element_type=f32)
    companions = jnp.concatenate([by_owner, before_user.astype(bf16)[:, None, :]], axis=1)
    same = jnp.einsum("ujo,uko->ujk", by_owner, companions, preferred_element_type=f32)
    slot_ids = lax.broadcasted_iota(jnp.int32, (history_length, history_length + 1), 0)
    other_ids = lax.broadcasted_iota(jnp.int32, (history_length, history_length + 1), 1)
    counted = ((other_ids < slot_ids) | (other_ids == history_length)).astype(f32)
    ranks = jnp.einsum("ujk,jk->uj", same, counted).astype(jnp.int32).reshape(lookups)

    flat_rows = local_rows.reshape(lookups, 1)
    row_high = flat_rows // 32
    row_low = flat_rows - row_high * 32
    user_of = lax.broadcasted_iota(jnp.int32, (user_count, history_length), 0).reshape(lookups, 1)
    flat_live = live.reshape(lookups, 1)
    columns = lax.broadcasted_iota(jnp.int32, (lookups, 4 * capacity), 1)
    part = columns // capacity
    chosen = (columns - part * capacity == ranks[:, None]) & flat_live
    value = jnp.where(
        part == 0, row_high, jnp.where(part == 1, row_low, jnp.where(part == 2, user_of, 1))
    )
    spread = jnp.where(chosen, value, 0).astype(bf16)
    slots = jnp.einsum(
        "io,ic->oc", by_owner.reshape(lookups, devices), spread, preferred_element_type=f32
    ).reshape(devices, 4, capacity)
    slots = slots.astype(jnp.int32)
    requests = slots[:, 0] * 32 + slots[:, 1]
    slot_user = slots[:, 2].reshape(slots_total)
    slot_used = slots[:, 3].reshape(slots_total)


    gram_width = embed_width * embed_width // devices
    outgoing = jnp.concatenate(
        [requests.astype(f32), local_gram.reshape(devices, gram_width)], axis=1
    )
    received = exchange(outgoing)
    incoming = received[:, :capacity].astype(jnp.int32).reshape(slots_total)
    gram_slice = jnp.sum(received[:, capacity:], axis=0)
    high = lax.optimization_barrier(gram_slice.astype(bf16))
    rest = gram_slice - high.astype(f32)
    middle = lax.optimization_barrier(rest.astype(bf16))
    low = (rest - middle.astype(f32)).astype(bf16)
    pieces = jnp.concatenate([high, middle, low], axis=0)
    extra_rows = -(-pieces.shape[0] // embed_width)
    pieces = jnp.pad(pieces, (0, extra_rows * embed_width - pieces.shape[0]))
    source_rows = jnp.concatenate(
        [item_table.astype(f32), pieces.astype(f32).reshape(extra_rows, embed_width)], axis=0
    )
    reply_capacity = capacity + extra_rows
    answered = answer_rows(source_rows, incoming, devices, reply_capacity, bf16)
    replies = exchange(answered)
    parts = replies[:, capacity:].reshape(devices, extra_rows * embed_width)[:, : 3 * gram_width]
    parts = parts.astype(f32).reshape(devices, 3, gram_width)
    gramian = ((parts[:, 0] + parts[:, 1]) + parts[:, 2]).reshape(embed_width, embed_width)
    fetched = fetch_rows(replies, owners.reshape(lookups), ranks).reshape(
        user_count, history_length, embed_width
    )
    weights = live.astype(f32)
    narrow_weights = weights.astype(bf16)
    target = jnp.einsum("ul,ulk->uk", narrow_weights, fetched, preferred_element_type=f32)
    unseen_scale = unobserved_weight / (table_rows * devices)
    solution = jnp.zeros_like(target)
    residual = target
    direction = target
    norm_now = jnp.sum(residual * residual, axis=1)
    for iteration in range(ITERS):
        narrow = direction.astype(bf16)
        scores = jnp.einsum("ulk,uk->ul", fetched, narrow, preferred_element_type=f32)
        scores = (scores * weights).astype(bf16)
        returned = jnp.einsum("ulk,ul->uk", fetched, scores, preferred_element_type=f32)
        curved = jnp.dot(direction, gramian, precision=lax.Precision.HIGHEST)
        applied = unseen_scale * curved + returned + ridge * direction
        step_size = norm_now / jnp.sum(direction * applied, axis=1)
        solution = solution + step_size[:, None] * direction
        residual = residual - step_size[:, None] * applied
        norm_next = jnp.sum(residual * residual, axis=1)
        direction = residual + (norm_next / norm_now)[:, None] * direction
        norm_now = norm_next

    member_ids = lax.broadcasted_iota(jnp.int32, (slots_total, user_count), 1)
    member = ((slot_user[:, None] == member_ids) & (slot_used[:, None] > 0)).astype(bf16)
    partials = jnp.einsum("su,uk->sk", member, solution.astype(bf16), preferred_element_type=f32)
    partials = partials.astype(bf16).reshape(devices, capacity, embed_width)
    arrived = exchange(partials).reshape(slots_total, embed_width)
    table_ids = lax.broadcasted_iota(jnp.int32, (slots_total, table_rows), 1)
    picks = (incoming[:, None] == table_ids).astype(bf16)
    item_rhs = jnp.einsum("st,sk->tk", picks, arrived, preferred_element_type=f32)
    return (solution, item_rhs)


def solution(mesh):
    return jax.shard_map(
        on_device,
        mesh=mesh,
        in_specs=(P(("rows", "grp"), None), P(("rows", "grp"), None), P(("rows", "grp"))),
        out_specs=(P(("rows", "grp"), None), P(("rows", "grp"), None)),
        check_vma=False,
    )
```

```python
import jax
import jax.numpy as jnp
from jax import lax
from jax.experimental import pallas as pl
from jax.experimental.pallas import tpu as pltpu
from jax.sharding import PartitionSpec as P

ITERS = 3


unobserved_weight = 25.0
ridge = 0.1


def exchange(values):
    return lax.all_to_all(values, ("rows", "grp"), 0, 0, tiled=True)


def sum_over_devices(value):
    for axis in ("grp", "rows"):
        size = lax.axis_size(axis)
        stride = 1
        while stride < size:
            partners = [(i, i ^ stride) for i in range(size)]
            value = value + lax.ppermute(value, axis, partners)
            stride *= 2
    return value


GATHER_TILE = 16


def gather_rows_kernel(index_ref, source_ref, out_ref):
    def body(tile, carry):
        first = pl.multiple_of(tile * GATHER_TILE, GATHER_TILE)
        rows = [source_ref[pl.ds(index_ref[first + r], 1), :] for r in range(GATHER_TILE)]
        out_ref[pl.ds(first, GATHER_TILE), :] = jnp.concatenate(rows, axis=0).astype(out_ref.dtype)
        return carry

    lax.fori_loop(0, out_ref.shape[0] // GATHER_TILE, body, 0, unroll=8)


def gather_rows(wide, index, dtype):
    count = index.shape[0]
    rows, width = wide.shape
    picked = pl.pallas_call(
        gather_rows_kernel,
        grid_spec=pltpu.PrefetchScalarGridSpec(
            num_scalar_prefetch=1,
            grid=(1,),
            in_specs=[pl.BlockSpec((rows, width), lambda i, index_ref: (0, 0))],
            out_specs=pl.BlockSpec((count, width), lambda i, index_ref: (0, 0)),
        ),
        out_shape=jax.ShapeDtypeStruct((count, width), dtype),
    )(index, wide)
    return picked


def answer_kernel(index_ref, source_ref, out_ref):
    chunks, depth, _ = out_ref.shape
    capacity = index_ref.shape[0] // chunks
    table_rows = source_ref.shape[0] - (depth - capacity)
    extra = source_ref[pl.ds(table_rows, depth - capacity), :].astype(out_ref.dtype)

    def body(chunk, carry):
        for start in range(0, capacity, GATHER_TILE):
            first = chunk * capacity + start
            rows = [source_ref[pl.ds(index_ref[first + r], 1), :] for r in range(GATHER_TILE)]
            out_ref[chunk, pl.ds(start, GATHER_TILE), :] = jnp.concatenate(rows, axis=0).astype(
                out_ref.dtype
            )
        out_ref[chunk, pl.ds(capacity, depth - capacity), :] = extra
        return carry

    lax.fori_loop(0, chunks, body, 0, unroll=4)


def answer_rows(wide, index, chunks, depth, dtype):
    rows, width = wide.shape
    return pl.pallas_call(
        answer_kernel,
        grid_spec=pltpu.PrefetchScalarGridSpec(
            num_scalar_prefetch=1,
            grid=(1,),
            in_specs=[pl.BlockSpec((rows, width), lambda i, index_ref: (0, 0))],
            out_specs=pl.BlockSpec((chunks, depth, width), lambda i, index_ref: (0, 0, 0)),
        ),
        out_shape=jax.ShapeDtypeStruct((chunks, depth, width), dtype),
    )(index, wide)


def on_device(item_table, histories, counts):
    row_count = lax.axis_size("rows")
    group_count = lax.axis_size("grp")
    devices = row_count * group_count
    table_rows, embed_width = item_table.shape
    user_count, history_length = histories.shape
    lookups = user_count * history_length
    capacity = max(4, 2 * lookups // devices)
    slots_total = devices * capacity
    bf16 = jnp.bfloat16
    f32 = jnp.float32

    local_gram = lax.dot_general(
        item_table, item_table, (((0,), (0,)), ((), ())), preferred_element_type=f32
    )

    positions = lax.broadcasted_iota(jnp.int32, (user_count, history_length), 1)
    live = positions < counts[:, None]
    owners = histories // table_rows
    local_rows = histories - owners * table_rows
    owner_ids = lax.broadcasted_iota(jnp.int32, (user_count, history_length, devices), 2)
    by_owner = ((owners[:, :, None] == owner_ids) & live[:, :, None]).astype(bf16)
    per_user = jnp.sum(by_owner.astype(f32), axis=1)
    user_ids = lax.broadcasted_iota(jnp.int32, (user_count, user_count), 0)
    earlier_users = (lax.broadcasted_iota(jnp.int32, (user_count, user_count), 1) < user_ids).astype(bf16)
    before_user = jnp.einsum("uv,vo->uo", earlier_users, per_user.astype(bf16), preferred_element_type=f32)
    companions = jnp.concatenate([by_owner, before_user.astype(bf16)[:, None, :]], axis=1)
    same = jnp.einsum("ujo,uko->ujk", by_owner, companions, preferred_element_type=f32)
    slot_ids = lax.broadcasted_iota(jnp.int32, (history_length, history_length + 1), 0)
    other_ids = lax.broadcasted_iota(jnp.int32, (history_length, history_length + 1), 1)
    counted = ((other_ids < slot_ids) | (other_ids == history_length)).astype(f32)
    ranks = jnp.einsum("ujk,jk->uj", same, counted).astype(jnp.int32).reshape(lookups)

    flat_rows = local_rows.reshape(lookups, 1)
    row_high = flat_rows // 32
    row_low = flat_rows - row_high * 32
    user_of = lax.broadcasted_iota(jnp.int32, (user_count, history_length), 0).reshape(lookups, 1)
    flat_live = live.reshape(lookups, 1)
    columns = lax.broadcasted_iota(jnp.int32, (lookups, 4 * capacity), 1)
    part = columns // capacity
    chosen = (columns - part * capacity == ranks[:, None]) & flat_live
    value = jnp.where(
        part == 0, row_high, jnp.where(part == 1, row_low, jnp.where(part == 2, user_of, 1))
    )
    spread = jnp.where(chosen, value, 0).astype(bf16)
    slots = jnp.einsum(
        "io,ic->oc", by_owner.reshape(lookups, devices), spread, preferred_element_type=f32
    ).reshape(devices, 4, capacity)
    slots = slots.astype(jnp.int32)
    requests = slots[:, 0] * 32 + slots[:, 1]
    slot_user = slots[:, 2].reshape(slots_total)
    slot_used = slots[:, 3].reshape(slots_total)


    gram_width = embed_width * embed_width // devices
    outgoing = jnp.concatenate(
        [requests.astype(f32), local_gram.reshape(devices, gram_width)], axis=1
    )
    received = exchange(outgoing)
    incoming = received[:, :capacity].astype(jnp.int32).reshape(slots_total)
    gram_slice = jnp.sum(received[:, capacity:], axis=0)
    high = lax.optimization_barrier(gram_slice.astype(bf16))
    rest = gram_slice - high.astype(f32)
    middle = lax.optimization_barrier(rest.astype(bf16))
    low = (rest - middle.astype(f32)).astype(bf16)
    pieces = jnp.concatenate([high, middle, low], axis=0)
    extra_rows = -(-pieces.shape[0] // embed_width)
    pieces = jnp.pad(pieces, (0, extra_rows * embed_width - pieces.shape[0]))
    source_rows = jnp.concatenate(
        [item_table.astype(f32), pieces.astype(f32).reshape(extra_rows, embed_width)], axis=0
    )
    reply_capacity = capacity + extra_rows
    answered = answer_rows(source_rows, incoming, devices, reply_capacity, bf16)
    replies = exchange(answered)
    parts = replies[:, capacity:].reshape(devices, extra_rows * embed_width)[:, : 3 * gram_width]
    parts = parts.astype(f32).reshape(devices, 3, gram_width)
    gramian = ((parts[:, 0] + parts[:, 1]) + parts[:, 2]).reshape(embed_width, embed_width)
    reply_rows = replies.reshape(devices * reply_capacity, embed_width)
    slot_index = owners.reshape(lookups) * reply_capacity + ranks
    fetched = gather_rows(reply_rows.astype(f32), slot_index, bf16).reshape(
        user_count, history_length, embed_width
    )
    weights = live.astype(f32)
    narrow_weights = weights.astype(bf16)
    target = jnp.einsum("ul,ulk->uk", narrow_weights, fetched, preferred_element_type=f32)
    unseen_scale = unobserved_weight / (table_rows * devices)
    solution = jnp.zeros_like(target)
    residual = target
    direction = target
    norm_now = jnp.sum(residual * residual, axis=1)
    for iteration in range(ITERS):
        narrow = direction.astype(bf16)
        scores = jnp.einsum("ulk,uk->ul", fetched, narrow, preferred_element_type=f32)
        scores = (scores * weights).astype(bf16)
        returned = jnp.einsum("ulk,ul->uk", fetched, scores, preferred_element_type=f32)
        curved = jnp.dot(direction, gramian, precision=lax.Precision.HIGHEST)
        applied = unseen_scale * curved + returned + ridge * direction
        step_size = norm_now / jnp.sum(direction * applied, axis=1)
        solution = solution + step_size[:, None] * direction
        residual = residual - step_size[:, None] * applied
        norm_next = jnp.sum(residual * residual, axis=1)
        direction = residual + (norm_next / norm_now)[:, None] * direction
        norm_now = norm_next

    member_ids = lax.broadcasted_iota(jnp.int32, (slots_total, user_count), 1)
    member = ((slot_user[:, None] == member_ids) & (slot_used[:, None] > 0)).astype(bf16)
    partials = jnp.einsum("su,uk->sk", member, solution.astype(bf16), preferred_element_type=f32)
    partials = partials.astype(bf16).reshape(devices, capacity, embed_width)
    arrived = exchange(partials).reshape(slots_total, embed_width)
    table_ids = lax.broadcasted_iota(jnp.int32, (table_rows, slots_total), 0)
    picks = (table_ids == incoming[None, :]).astype(bf16)
    item_rhs = jnp.dot(picks, arrived, preferred_element_type=f32)
    return (solution, item_rhs)


def solution(mesh):
    return jax.shard_map(
        on_device,
        mesh=mesh,
        in_specs=(P(("rows", "grp"), None), P(("rows", "grp"), None), P(("rows", "grp"))),
        out_specs=(P(("rows", "grp"), None), P(("rows", "grp"), None)),
        check_vma=False,
    )
```

```python
import jax
import jax.numpy as jnp
from jax import lax
from jax.experimental import pallas as pl
from jax.experimental.pallas import tpu as pltpu
from jax.sharding import PartitionSpec as P

ITERS = 3


unobserved_weight = 25.0
ridge = 0.1


def exchange(values):
    return lax.all_to_all(values, ("rows", "grp"), 0, 0, tiled=True)


def sum_over_devices(value):
    for axis in ("grp", "rows"):
        size = lax.axis_size(axis)
        stride = 1
        while stride < size:
            partners = [(i, i ^ stride) for i in range(size)]
            value = value + lax.ppermute(value, axis, partners)
            stride *= 2
    return value


GATHER_TILE = 16


def gather_rows_kernel(index_ref, source_ref, out_ref):
    def body(tile, carry):
        first = pl.multiple_of(tile * GATHER_TILE, GATHER_TILE)
        rows = [source_ref[pl.ds(index_ref[first + r], 1), :] for r in range(GATHER_TILE)]
        out_ref[pl.ds(first, GATHER_TILE), :] = jnp.concatenate(rows, axis=0).astype(out_ref.dtype)
        return carry

    lax.fori_loop(0, out_ref.shape[0] // GATHER_TILE, body, 0, unroll=8)


def gather_rows(wide, index, dtype):
    count = index.shape[0]
    rows, width = wide.shape
    picked = pl.pallas_call(
        gather_rows_kernel,
        grid_spec=pltpu.PrefetchScalarGridSpec(
            num_scalar_prefetch=1,
            grid=(1,),
            in_specs=[pl.BlockSpec((rows, width), lambda i, index_ref: (0, 0))],
            out_specs=pl.BlockSpec((count, width), lambda i, index_ref: (0, 0)),
        ),
        out_shape=jax.ShapeDtypeStruct((count, width), dtype),
    )(index, wide)
    return picked


def answer_kernel(index_ref, source_ref, out_ref):
    chunks, depth, _ = out_ref.shape
    capacity = index_ref.shape[0] // chunks
    table_rows = source_ref.shape[0] - (depth - capacity)
    extra = source_ref[pl.ds(table_rows, depth - capacity), :].astype(out_ref.dtype)

    def body(chunk, carry):
        for start in range(0, capacity, GATHER_TILE):
            first = chunk * capacity + start
            rows = [source_ref[pl.ds(index_ref[first + r], 1), :] for r in range(GATHER_TILE)]
            out_ref[chunk, pl.ds(start, GATHER_TILE), :] = jnp.concatenate(rows, axis=0).astype(
                out_ref.dtype
            )
        out_ref[chunk, pl.ds(capacity, depth - capacity), :] = extra
        return carry

    lax.fori_loop(0, chunks, body, 0, unroll=4)


def answer_rows(wide, index, chunks, depth, dtype):
    rows, width = wide.shape
    return pl.pallas_call(
        answer_kernel,
        grid_spec=pltpu.PrefetchScalarGridSpec(
            num_scalar_prefetch=1,
            grid=(1,),
            in_specs=[pl.BlockSpec((rows, width), lambda i, index_ref: (0, 0))],
            out_specs=pl.BlockSpec((chunks, depth, width), lambda i, index_ref: (0, 0, 0)),
        ),
        out_shape=jax.ShapeDtypeStruct((chunks, depth, width), dtype),
    )(index, wide)


def on_device(item_table, histories, counts):
    row_count = lax.axis_size("rows")
    group_count = lax.axis_size("grp")
    devices = row_count * group_count
    table_rows, embed_width = item_table.shape
    user_count, history_length = histories.shape
    lookups = user_count * history_length
    capacity = max(4, 2 * lookups // devices)
    slots_total = devices * capacity
    bf16 = jnp.bfloat16
    f32 = jnp.float32

    local_gram = lax.dot_general(
        item_table, item_table, (((0,), (0,)), ((), ())), preferred_element_type=f32
    )

    positions = lax.broadcasted_iota(jnp.int32, (user_count, history_length), 1)
    live = positions < counts[:, None]
    owners = histories // table_rows
    local_rows = histories - owners * table_rows
    owner_ids = lax.broadcasted_iota(jnp.int32, (user_count, history_length, devices), 2)
    by_owner = ((owners[:, :, None] == owner_ids) & live[:, :, None]).astype(bf16)
    per_user = jnp.sum(by_owner.astype(f32), axis=1)
    user_ids = lax.broadcasted_iota(jnp.int32, (user_count, user_count), 0)
    earlier_users = (lax.broadcasted_iota(jnp.int32, (user_count, user_count), 1) < user_ids).astype(bf16)
    before_user = jnp.einsum("uv,vo->uo", earlier_users, per_user.astype(bf16), preferred_element_type=f32)
    companions = jnp.concatenate([by_owner, before_user.astype(bf16)[:, None, :]], axis=1)
    same = jnp.einsum("ujo,uko->ujk", by_owner, companions, preferred_element_type=f32)
    slot_ids = lax.broadcasted_iota(jnp.int32, (history_length, history_length + 1), 0)
    other_ids = lax.broadcasted_iota(jnp.int32, (history_length, history_length + 1), 1)
    counted = ((other_ids < slot_ids) | (other_ids == history_length)).astype(f32)
    ranks = jnp.einsum("ujk,jk->uj", same, counted).astype(jnp.int32).reshape(lookups)

    flat_rows = local_rows.reshape(lookups, 1)
    row_high = flat_rows // 32
    row_low = flat_rows - row_high * 32
    user_of = lax.broadcasted_iota(jnp.int32, (user_count, history_length), 0).reshape(lookups, 1)
    flat_live = live.reshape(lookups, 1)
    columns = lax.broadcasted_iota(jnp.int32, (lookups, 4 * capacity), 1)
    part = columns // capacity
    chosen = (columns - part * capacity == ranks[:, None]) & flat_live
    value = jnp.where(
        part == 0, row_high, jnp.where(part == 1, row_low, jnp.where(part == 2, user_of, 1))
    )
    spread = jnp.where(chosen, value, 0).astype(bf16)
    slots = jnp.einsum(
        "io,ic->oc", by_owner.reshape(lookups, devices), spread, preferred_element_type=f32
    ).reshape(devices, 4, capacity)
    slots = slots.astype(jnp.int32)
    requests = slots[:, 0] * 32 + slots[:, 1]
    slot_user = slots[:, 2].reshape(slots_total)
    slot_used = slots[:, 3].reshape(slots_total)


    gram_width = embed_width * embed_width // devices
    outgoing = jnp.concatenate(
        [requests.astype(f32), local_gram.reshape(devices, gram_width)], axis=1
    )
    received = exchange(outgoing)
    incoming = received[:, :capacity].astype(jnp.int32).reshape(slots_total)
    gram_slice = jnp.sum(received[:, capacity:], axis=0)
    high = lax.optimization_barrier(gram_slice.astype(bf16))
    rest = gram_slice - high.astype(f32)
    middle = lax.optimization_barrier(rest.astype(bf16))
    low = (rest - middle.astype(f32)).astype(bf16)
    pieces = jnp.concatenate([high, middle, low], axis=0)
    extra_rows = -(-pieces.shape[0] // embed_width)
    pieces = jnp.pad(pieces, (0, extra_rows * embed_width - pieces.shape[0]))
    source_rows = jnp.concatenate(
        [item_table.astype(f32), pieces.astype(f32).reshape(extra_rows, embed_width)], axis=0
    )
    reply_capacity = capacity + extra_rows
    answered = answer_rows(source_rows, incoming, devices, reply_capacity, bf16)
    replies = exchange(answered)
    table_ids = lax.broadcasted_iota(jnp.int32, (table_rows, slots_total), 0)
    picks = lax.optimization_barrier((table_ids == incoming[None, :]).astype(bf16))
    parts = replies[:, capacity:].reshape(devices, extra_rows * embed_width)[:, : 3 * gram_width]
    parts = parts.astype(f32).reshape(devices, 3, gram_width)
    gramian = ((parts[:, 0] + parts[:, 1]) + parts[:, 2]).reshape(embed_width, embed_width)
    reply_rows = replies.reshape(devices * reply_capacity, embed_width)
    slot_index = owners.reshape(lookups) * reply_capacity + ranks
    fetched = gather_rows(reply_rows.astype(f32), slot_index, bf16).reshape(
        user_count, history_length, embed_width
    )
    weights = live.astype(f32)
    narrow_weights = weights.astype(bf16)
    target = jnp.einsum("ul,ulk->uk", narrow_weights, fetched, preferred_element_type=f32)
    unseen_scale = unobserved_weight / (table_rows * devices)
    solution = jnp.zeros_like(target)
    residual = target
    direction = target
    norm_now = jnp.sum(residual * residual, axis=1)
    for iteration in range(ITERS):
        narrow = direction.astype(bf16)
        scores = jnp.einsum("ulk,uk->ul", fetched, narrow, preferred_element_type=f32)
        scores = (scores * weights).astype(bf16)
        returned = jnp.einsum("ulk,ul->uk", fetched, scores, preferred_element_type=f32)
        curved = jnp.dot(direction, gramian, precision=lax.Precision.HIGHEST)
        applied = unseen_scale * curved + returned + ridge * direction
        step_size = norm_now / jnp.sum(direction * applied, axis=1)
        solution = solution + step_size[:, None] * direction
        residual = residual - step_size[:, None] * applied
        norm_next = jnp.sum(residual * residual, axis=1)
        direction = residual + (norm_next / norm_now)[:, None] * direction
        norm_now = norm_next

    member_ids = lax.broadcasted_iota(jnp.int32, (slots_total, user_count), 1)
    member = ((slot_user[:, None] == member_ids) & (slot_used[:, None] > 0)).astype(bf16)
    partials = jnp.einsum("su,uk->sk", member, solution.astype(bf16), preferred_element_type=f32)
    partials = partials.astype(bf16).reshape(devices, capacity, embed_width)
    arrived = exchange(partials).reshape(slots_total, embed_width)
    item_rhs = jnp.dot(picks, arrived, preferred_element_type=f32)
    return (solution, item_rhs)


def solution(mesh):
    return jax.shard_map(
        on_device,
        mesh=mesh,
        in_specs=(P(("rows", "grp"), None), P(("rows", "grp"), None), P(("rows", "grp"))),
        out_specs=(P(("rows", "grp"), None), P(("rows", "grp"), None)),
        check_vma=False,
    )
```

```python
import jax
import jax.numpy as jnp
from jax import lax
from jax.experimental import pallas as pl
from jax.experimental.pallas import tpu as pltpu
from jax.sharding import PartitionSpec as P

ITERS = 3


unobserved_weight = 25.0
ridge = 0.1


def exchange(values):
    return lax.all_to_all(values, ("rows", "grp"), 0, 0, tiled=True)


def sum_over_devices(value):
    for axis in ("grp", "rows"):
        size = lax.axis_size(axis)
        stride = 1
        while stride < size:
            partners = [(i, i ^ stride) for i in range(size)]
            value = value + lax.ppermute(value, axis, partners)
            stride *= 2
    return value


GATHER_TILE = 32


def gather_rows_kernel(index_ref, source_ref, out_ref):
    def body(tile, carry):
        first = pl.multiple_of(tile * GATHER_TILE, GATHER_TILE)
        rows = [source_ref[pl.ds(index_ref[first + r], 1), :] for r in range(GATHER_TILE)]
        out_ref[pl.ds(first, GATHER_TILE), :] = jnp.concatenate(rows, axis=0).astype(out_ref.dtype)
        return carry

    lax.fori_loop(0, out_ref.shape[0] // GATHER_TILE, body, 0, unroll=8)


def gather_rows(wide, index, dtype):
    count = index.shape[0]
    rows, width = wide.shape
    picked = pl.pallas_call(
        gather_rows_kernel,
        grid_spec=pltpu.PrefetchScalarGridSpec(
            num_scalar_prefetch=1,
            grid=(1,),
            in_specs=[pl.BlockSpec((rows, width), lambda i, index_ref: (0, 0))],
            out_specs=pl.BlockSpec((count, width), lambda i, index_ref: (0, 0)),
        ),
        out_shape=jax.ShapeDtypeStruct((count, width), dtype),
    )(index, wide)
    return picked


def answer_kernel(index_ref, source_ref, out_ref):
    chunks, depth, _ = out_ref.shape
    capacity = index_ref.shape[0] // chunks
    table_rows = source_ref.shape[0] - (depth - capacity)
    extra = source_ref[pl.ds(table_rows, depth - capacity), :].astype(out_ref.dtype)

    def body(chunk, carry):
        for start in range(0, capacity, GATHER_TILE):
            first = chunk * capacity + start
            rows = [source_ref[pl.ds(index_ref[first + r], 1), :] for r in range(GATHER_TILE)]
            out_ref[chunk, pl.ds(start, GATHER_TILE), :] = jnp.concatenate(rows, axis=0).astype(
                out_ref.dtype
            )
        out_ref[chunk, pl.ds(capacity, depth - capacity), :] = extra
        return carry

    lax.fori_loop(0, chunks, body, 0, unroll=4)


def answer_rows(wide, index, chunks, depth, dtype):
    rows, width = wide.shape
    return pl.pallas_call(
        answer_kernel,
        grid_spec=pltpu.PrefetchScalarGridSpec(
            num_scalar_prefetch=1,
            grid=(1,),
            in_specs=[pl.BlockSpec((rows, width), lambda i, index_ref: (0, 0))],
            out_specs=pl.BlockSpec((chunks, depth, width), lambda i, index_ref: (0, 0, 0)),
        ),
        out_shape=jax.ShapeDtypeStruct((chunks, depth, width), dtype),
    )(index, wide)


def on_device(item_table, histories, counts):
    row_count = lax.axis_size("rows")
    group_count = lax.axis_size("grp")
    devices = row_count * group_count
    table_rows, embed_width = item_table.shape
    user_count, history_length = histories.shape
    lookups = user_count * history_length
    capacity = max(4, 2 * lookups // devices)
    slots_total = devices * capacity
    bf16 = jnp.bfloat16
    f32 = jnp.float32

    local_gram = lax.dot_general(
        item_table, item_table, (((0,), (0,)), ((), ())), preferred_element_type=f32
    )

    positions = lax.broadcasted_iota(jnp.int32, (user_count, history_length), 1)
    live = positions < counts[:, None]
    owners = histories // table_rows
    local_rows = histories - owners * table_rows
    owner_ids = lax.broadcasted_iota(jnp.int32, (user_count, history_length, devices), 2)
    by_owner = ((owners[:, :, None] == owner_ids) & live[:, :, None]).astype(bf16)
    per_user = jnp.sum(by_owner.astype(f32), axis=1)
    user_ids = lax.broadcasted_iota(jnp.int32, (user_count, user_count), 0)
    earlier_users = (lax.broadcasted_iota(jnp.int32, (user_count, user_count), 1) < user_ids).astype(bf16)
    before_user = jnp.einsum("uv,vo->uo", earlier_users, per_user.astype(bf16), preferred_element_type=f32)
    companions = jnp.concatenate([by_owner, before_user.astype(bf16)[:, None, :]], axis=1)
    same = jnp.einsum("ujo,uko->ujk", by_owner, companions, preferred_element_type=f32)
    slot_ids = lax.broadcasted_iota(jnp.int32, (history_length, history_length + 1), 0)
    other_ids = lax.broadcasted_iota(jnp.int32, (history_length, history_length + 1), 1)
    counted = ((other_ids < slot_ids) | (other_ids == history_length)).astype(f32)
    ranks = jnp.einsum("ujk,jk->uj", same, counted).astype(jnp.int32).reshape(lookups)

    flat_rows = local_rows.reshape(lookups, 1)
    row_high = flat_rows // 32
    row_low = flat_rows - row_high * 32
    user_of = lax.broadcasted_iota(jnp.int32, (user_count, history_length), 0).reshape(lookups, 1)
    flat_live = live.reshape(lookups, 1)
    columns = lax.broadcasted_iota(jnp.int32, (lookups, 4 * capacity), 1)
    part = columns // capacity
    chosen = (columns - part * capacity == ranks[:, None]) & flat_live
    value = jnp.where(
        part == 0, row_high, jnp.where(part == 1, row_low, jnp.where(part == 2, user_of, 1))
    )
    spread = jnp.where(chosen, value, 0).astype(bf16)
    slots = jnp.einsum(
        "io,ic->oc", by_owner.reshape(lookups, devices), spread, preferred_element_type=f32
    ).reshape(devices, 4, capacity)
    slots = slots.astype(jnp.int32)
    requests = slots[:, 0] * 32 + slots[:, 1]
    slot_user = slots[:, 2].reshape(slots_total)
    slot_used = slots[:, 3].reshape(slots_total)


    gram_width = embed_width * embed_width // devices
    outgoing = jnp.concatenate(
        [requests.astype(f32), local_gram.reshape(devices, gram_width)], axis=1
    )
    received = exchange(outgoing)
    incoming = received[:, :capacity].astype(jnp.int32).reshape(slots_total)
    gram_slice = jnp.sum(received[:, capacity:], axis=0)
    high = lax.optimization_barrier(gram_slice.astype(bf16))
    rest = gram_slice - high.astype(f32)
    middle = lax.optimization_barrier(rest.astype(bf16))
    low = (rest - middle.astype(f32)).astype(bf16)
    pieces = jnp.concatenate([high, middle, low], axis=0)
    extra_rows = -(-pieces.shape[0] // embed_width)
    pieces = jnp.pad(pieces, (0, extra_rows * embed_width - pieces.shape[0]))
    source_rows = jnp.concatenate(
        [item_table.astype(f32), pieces.astype(f32).reshape(extra_rows, embed_width)], axis=0
    )
    reply_capacity = capacity + extra_rows
    answered = answer_rows(source_rows, incoming, devices, reply_capacity, bf16)
    replies = exchange(answered)
    parts = replies[:, capacity:].reshape(devices, extra_rows * embed_width)[:, : 3 * gram_width]
    parts = parts.astype(f32).reshape(devices, 3, gram_width)
    gramian = ((parts[:, 0] + parts[:, 1]) + parts[:, 2]).reshape(embed_width, embed_width)
    reply_rows = replies.reshape(devices * reply_capacity, embed_width)
    slot_index = owners.reshape(lookups) * reply_capacity + ranks
    fetched = gather_rows(reply_rows.astype(f32), slot_index, bf16).reshape(
        user_count, history_length, embed_width
    )
    weights = live.astype(f32)
    narrow_weights = weights.astype(bf16)
    target = jnp.einsum("ul,ulk->uk", narrow_weights, fetched, preferred_element_type=f32)
    unseen_scale = unobserved_weight / (table_rows * devices)
    solution = jnp.zeros_like(target)
    residual = target
    direction = target
    norm_now = jnp.sum(residual * residual, axis=1)
    for iteration in range(ITERS):
        narrow = direction.astype(bf16)
        scores = jnp.einsum("ulk,uk->ul", fetched, narrow, preferred_element_type=f32)
        scores = (scores * weights).astype(bf16)
        returned = jnp.einsum("ulk,ul->uk", fetched, scores, preferred_element_type=f32)
        curved = jnp.dot(direction, gramian, precision=lax.Precision.HIGHEST)
        applied = unseen_scale * curved + returned + ridge * direction
        step_size = norm_now / jnp.sum(direction * applied, axis=1)
        solution = solution + step_size[:, None] * direction
        residual = residual - step_size[:, None] * applied
        norm_next = jnp.sum(residual * residual, axis=1)
        direction = residual + (norm_next / norm_now)[:, None] * direction
        norm_now = norm_next

    member_ids = lax.broadcasted_iota(jnp.int32, (slots_total, user_count), 1)
    member = ((slot_user[:, None] == member_ids) & (slot_used[:, None] > 0)).astype(bf16)
    partials = jnp.einsum("su,uk->sk", member, solution.astype(bf16), preferred_element_type=f32)
    partials = partials.astype(bf16).reshape(devices, capacity, embed_width)
    arrived = exchange(partials).reshape(slots_total, embed_width)
    table_ids = lax.broadcasted_iota(jnp.int32, (slots_total, table_rows), 1)
    picks = (incoming[:, None] == table_ids).astype(bf16)
    item_rhs = jnp.einsum("st,sk->tk", picks, arrived, preferred_element_type=f32)
    return (solution, item_rhs)


def solution(mesh):
    return jax.shard_map(
        on_device,
        mesh=mesh,
        in_specs=(P(("rows", "grp"), None), P(("rows", "grp"), None), P(("rows", "grp"))),
        out_specs=(P(("rows", "grp"), None), P(("rows", "grp"), None)),
        check_vma=False,
    )
```

```python
import jax
import jax.numpy as jnp
from jax import lax
from jax.experimental import pallas as pl
from jax.experimental.pallas import tpu as pltpu
from jax.sharding import PartitionSpec as P

ITERS = 3


unobserved_weight = 25.0
ridge = 0.1


def exchange(values):
    return lax.all_to_all(values, ("rows", "grp"), 0, 0, tiled=True)


def sum_over_devices(value):
    for axis in ("grp", "rows"):
        size = lax.axis_size(axis)
        stride = 1
        while stride < size:
            partners = [(i, i ^ stride) for i in range(size)]
            value = value + lax.ppermute(value, axis, partners)
            stride *= 2
    return value


GATHER_TILE = 16


def gather_rows_kernel(index_ref, source_ref, out_ref):
    def body(tile, carry):
        first = pl.multiple_of(tile * GATHER_TILE, GATHER_TILE)
        rows = [source_ref[pl.ds(index_ref[first + r], 1), :] for r in range(GATHER_TILE)]
        out_ref[pl.ds(first, GATHER_TILE), :] = jnp.concatenate(rows, axis=0).astype(out_ref.dtype)
        return carry

    lax.fori_loop(0, out_ref.shape[0] // GATHER_TILE, body, 0, unroll=8)


def gather_rows(wide, index, dtype):
    count = index.shape[0]
    rows, width = wide.shape
    picked = pl.pallas_call(
        gather_rows_kernel,
        grid_spec=pltpu.PrefetchScalarGridSpec(
            num_scalar_prefetch=1,
            grid=(1,),
            in_specs=[pl.BlockSpec((rows, width), lambda i, index_ref: (0, 0))],
            out_specs=pl.BlockSpec((count, width), lambda i, index_ref: (0, 0)),
        ),
        out_shape=jax.ShapeDtypeStruct((count, width), dtype),
    )(index, wide)
    return picked


def answer_kernel(index_ref, source_ref, out_ref):
    chunks, depth, _ = out_ref.shape
    capacity = index_ref.shape[0] // chunks
    table_rows = source_ref.shape[0] - (depth - capacity)
    extra = source_ref[pl.ds(table_rows, depth - capacity), :].astype(out_ref.dtype)

    def body(chunk, carry):
        for start in range(0, capacity, GATHER_TILE):
            first = chunk * capacity + start
            rows = [source_ref[pl.ds(index_ref[first + r], 1), :] for r in range(GATHER_TILE)]
            out_ref[chunk, pl.ds(start, GATHER_TILE), :] = jnp.concatenate(rows, axis=0).astype(
                out_ref.dtype
            )
        out_ref[chunk, pl.ds(capacity, depth - capacity), :] = extra
        return carry

    lax.fori_loop(0, chunks, body, 0, unroll=4)


def answer_rows(wide, index, chunks, depth, dtype):
    rows, width = wide.shape
    return pl.pallas_call(
        answer_kernel,
        grid_spec=pltpu.PrefetchScalarGridSpec(
            num_scalar_prefetch=1,
            grid=(1,),
            in_specs=[pl.BlockSpec((rows, width), lambda i, index_ref: (0, 0))],
            out_specs=pl.BlockSpec((chunks, depth, width), lambda i, index_ref: (0, 0, 0)),
        ),
        out_shape=jax.ShapeDtypeStruct((chunks, depth, width), dtype),
    )(index, wide)


def fetch_kernel(owner_ref, rank_ref, source_ref, out_ref):
    def body(tile, carry):
        first = pl.multiple_of(tile * GATHER_TILE, GATHER_TILE)
        rows = [
            source_ref[owner_ref[first + r], pl.ds(rank_ref[first + r], 1), :]
            for r in range(GATHER_TILE)
        ]
        out_ref[pl.ds(first, GATHER_TILE), :] = jnp.concatenate(rows, axis=0).astype(out_ref.dtype)
        return carry

    lax.fori_loop(0, out_ref.shape[0] // GATHER_TILE, body, 0, unroll=8)


def fetch_rows(source, owner, rank, dtype):
    count = owner.shape[0]
    return pl.pallas_call(
        fetch_kernel,
        grid_spec=pltpu.PrefetchScalarGridSpec(
            num_scalar_prefetch=2,
            grid=(1,),
            in_specs=[pl.BlockSpec(source.shape, lambda i, owner_ref, rank_ref: (0, 0, 0))],
            out_specs=pl.BlockSpec((count, source.shape[2]), lambda i, owner_ref, rank_ref: (0, 0)),
        ),
        out_shape=jax.ShapeDtypeStruct((count, source.shape[2]), dtype),
    )(owner, rank, source)


def on_device(item_table, histories, counts):
    row_count = lax.axis_size("rows")
    group_count = lax.axis_size("grp")
    devices = row_count * group_count
    table_rows, embed_width = item_table.shape
    user_count, history_length = histories.shape
    lookups = user_count * history_length
    capacity = max(4, 2 * lookups // devices)
    slots_total = devices * capacity
    bf16 = jnp.bfloat16
    f32 = jnp.float32

    local_gram = lax.dot_general(
        item_table, item_table, (((0,), (0,)), ((), ())), preferred_element_type=f32
    )

    positions = lax.broadcasted_iota(jnp.int32, (user_count, history_length), 1)
    live = positions < counts[:, None]
    owners = histories // table_rows
    local_rows = histories - owners * table_rows
    owner_ids = lax.broadcasted_iota(jnp.int32, (user_count, history_length, devices), 2)
    by_owner = ((owners[:, :, None] == owner_ids) & live[:, :, None]).astype(bf16)
    per_user = jnp.sum(by_owner.astype(f32), axis=1)
    user_ids = lax.broadcasted_iota(jnp.int32, (user_count, user_count), 0)
    earlier_users = (lax.broadcasted_iota(jnp.int32, (user_count, user_count), 1) < user_ids).astype(bf16)
    before_user = jnp.einsum("uv,vo->uo", earlier_users, per_user.astype(bf16), preferred_element_type=f32)
    companions = jnp.concatenate([by_owner, before_user.astype(bf16)[:, None, :]], axis=1)
    same = jnp.einsum("ujo,uko->ujk", by_owner, companions, preferred_element_type=f32)
    slot_ids = lax.broadcasted_iota(jnp.int32, (history_length, history_length + 1), 0)
    other_ids = lax.broadcasted_iota(jnp.int32, (history_length, history_length + 1), 1)
    counted = ((other_ids < slot_ids) | (other_ids == history_length)).astype(f32)
    ranks = jnp.einsum("ujk,jk->uj", same, counted).astype(jnp.int32).reshape(lookups)

    flat_rows = local_rows.reshape(lookups, 1)
    row_high = flat_rows // 32
    row_low = flat_rows - row_high * 32
    user_of = lax.broadcasted_iota(jnp.int32, (user_count, history_length), 0).reshape(lookups, 1)
    flat_live = live.reshape(lookups, 1)
    columns = lax.broadcasted_iota(jnp.int32, (lookups, 4 * capacity), 1)
    part = columns // capacity
    chosen = (columns - part * capacity == ranks[:, None]) & flat_live
    value = jnp.where(
        part == 0, row_high, jnp.where(part == 1, row_low, jnp.where(part == 2, user_of, 1))
    )
    spread = jnp.where(chosen, value, 0).astype(bf16)
    slots = jnp.einsum(
        "io,ic->oc", by_owner.reshape(lookups, devices), spread, preferred_element_type=f32
    ).reshape(devices, 4, capacity)
    slots = slots.astype(jnp.int32)
    requests = slots[:, 0] * 32 + slots[:, 1]
    slot_user = slots[:, 2].reshape(slots_total)
    slot_used = slots[:, 3].reshape(slots_total)


    gram_width = embed_width * embed_width // devices
    outgoing = jnp.concatenate(
        [requests.astype(f32), local_gram.reshape(devices, gram_width)], axis=1
    )
    received = exchange(outgoing)
    incoming = received[:, :capacity].astype(jnp.int32).reshape(slots_total)
    gram_slice = jnp.sum(received[:, capacity:], axis=0)
    high = lax.optimization_barrier(gram_slice.astype(bf16))
    rest = gram_slice - high.astype(f32)
    middle = lax.optimization_barrier(rest.astype(bf16))
    low = (rest - middle.astype(f32)).astype(bf16)
    pieces = jnp.concatenate([high, middle, low], axis=0)
    extra_rows = -(-pieces.shape[0] // embed_width)
    pieces = jnp.pad(pieces, (0, extra_rows * embed_width - pieces.shape[0]))
    source_rows = jnp.concatenate(
        [item_table.astype(f32), pieces.astype(f32).reshape(extra_rows, embed_width)], axis=0
    )
    reply_capacity = capacity + extra_rows
    answered = answer_rows(source_rows, incoming, devices, reply_capacity, bf16)
    replies = exchange(answered)
    parts = replies[:, capacity:].reshape(devices, extra_rows * embed_width)[:, : 3 * gram_width]
    parts = parts.astype(f32).reshape(devices, 3, gram_width)
    gramian = ((parts[:, 0] + parts[:, 1]) + parts[:, 2]).reshape(embed_width, embed_width)
    fetched = fetch_rows(replies.astype(f32), owners.reshape(lookups), ranks, bf16).reshape(
        user_count, history_length, embed_width
    )
    weights = live.astype(f32)
    narrow_weights = weights.astype(bf16)
    target = jnp.einsum("ul,ulk->uk", narrow_weights, fetched, preferred_element_type=f32)
    unseen_scale = unobserved_weight / (table_rows * devices)
    solution = jnp.zeros_like(target)
    residual = target
    direction = target
    norm_now = jnp.sum(residual * residual, axis=1)
    for iteration in range(ITERS):
        narrow = direction.astype(bf16)
        scores = jnp.einsum("ulk,uk->ul", fetched, narrow, preferred_element_type=f32)
        scores = (scores * weights).astype(bf16)
        returned = jnp.einsum("ulk,ul->uk", fetched, scores, preferred_element_type=f32)
        curved = jnp.dot(direction, gramian, precision=lax.Precision.HIGHEST)
        applied = unseen_scale * curved + returned + ridge * direction
        step_size = norm_now / jnp.sum(direction * applied, axis=1)
        solution = solution + step_size[:, None] * direction
        residual = residual - step_size[:, None] * applied
        norm_next = jnp.sum(residual * residual, axis=1)
        direction = residual + (norm_next / norm_now)[:, None] * direction
        norm_now = norm_next

    member_ids = lax.broadcasted_iota(jnp.int32, (slots_total, user_count), 1)
    member = ((slot_user[:, None] == member_ids) & (slot_used[:, None] > 0)).astype(bf16)
    partials = jnp.einsum("su,uk->sk", member, solution.astype(bf16), preferred_element_type=f32)
    partials = partials.astype(bf16).reshape(devices, capacity, embed_width)
    arrived = exchange(partials).reshape(slots_total, embed_width)
    table_ids = lax.broadcasted_iota(jnp.int32, (slots_total, table_rows), 1)
    picks = (incoming[:, None] == table_ids).astype(bf16)
    item_rhs = jnp.einsum("st,sk->tk", picks, arrived, preferred_element_type=f32)
    return (solution, item_rhs)


def solution(mesh):
    return jax.shard_map(
        on_device,
        mesh=mesh,
        in_specs=(P(("rows", "grp"), None), P(("rows", "grp"), None), P(("rows", "grp"))),
        out_specs=(P(("rows", "grp"), None), P(("rows", "grp"), None)),
        check_vma=False,
    )
```

```python
import jax
import jax.numpy as jnp
from jax import lax
from jax.experimental import pallas as pl
from jax.experimental.pallas import tpu as pltpu
from jax.sharding import PartitionSpec as P

ITERS = 3


unobserved_weight = 25.0
ridge = 0.1


def exchange(values):
    return lax.all_to_all(values, ("rows", "grp"), 0, 0, tiled=True)


def sum_over_devices(value):
    for axis in ("grp", "rows"):
        size = lax.axis_size(axis)
        stride = 1
        while stride < size:
            partners = [(i, i ^ stride) for i in range(size)]
            value = value + lax.ppermute(value, axis, partners)
            stride *= 2
    return value


GATHER_TILE = 16


def gather_rows_kernel(index_ref, source_ref, out_ref):
    def body(tile, carry):
        first = pl.multiple_of(tile * GATHER_TILE, GATHER_TILE)
        rows = [source_ref[pl.ds(index_ref[first + r], 1), :] for r in range(GATHER_TILE)]
        out_ref[pl.ds(first, GATHER_TILE), :] = jnp.concatenate(rows, axis=0).astype(out_ref.dtype)
        return carry

    lax.fori_loop(0, out_ref.shape[0] // GATHER_TILE, body, 0, unroll=8)


def gather_rows(wide, index, dtype):
    count = index.shape[0]
    rows, width = wide.shape
    picked = pl.pallas_call(
        gather_rows_kernel,
        grid_spec=pltpu.PrefetchScalarGridSpec(
            num_scalar_prefetch=1,
            grid=(1,),
            in_specs=[pl.BlockSpec((rows, width), lambda i, index_ref: (0, 0))],
            out_specs=pl.BlockSpec((count, width), lambda i, index_ref: (0, 0)),
        ),
        out_shape=jax.ShapeDtypeStruct((count, width), dtype),
    )(index, wide)
    return picked


def answer_kernel(index_ref, source_ref, out_ref):
    chunks, depth, _ = out_ref.shape
    capacity = index_ref.shape[0] // chunks
    table_rows = source_ref.shape[0] - (depth - capacity)
    extra = source_ref[pl.ds(table_rows, depth - capacity), :].astype(out_ref.dtype)

    def body(chunk, carry):
        for start in range(0, capacity, GATHER_TILE):
            first = chunk * capacity + start
            rows = [source_ref[pl.ds(index_ref[first + r], 1), :] for r in range(GATHER_TILE)]
            out_ref[chunk, pl.ds(start, GATHER_TILE), :] = jnp.concatenate(rows, axis=0).astype(
                out_ref.dtype
            )
        out_ref[chunk, pl.ds(capacity, depth - capacity), :] = extra
        return carry

    lax.fori_loop(0, chunks, body, 0, unroll=8)


def answer_rows(wide, index, chunks, depth, dtype):
    rows, width = wide.shape
    return pl.pallas_call(
        answer_kernel,
        grid_spec=pltpu.PrefetchScalarGridSpec(
            num_scalar_prefetch=1,
            grid=(1,),
            in_specs=[pl.BlockSpec((rows, width), lambda i, index_ref: (0, 0))],
            out_specs=pl.BlockSpec((chunks, depth, width), lambda i, index_ref: (0, 0, 0)),
        ),
        out_shape=jax.ShapeDtypeStruct((chunks, depth, width), dtype),
    )(index, wide)


def on_device(item_table, histories, counts):
    row_count = lax.axis_size("rows")
    group_count = lax.axis_size("grp")
    devices = row_count * group_count
    table_rows, embed_width = item_table.shape
    user_count, history_length = histories.shape
    lookups = user_count * history_length
    capacity = max(4, 2 * lookups // devices)
    slots_total = devices * capacity
    bf16 = jnp.bfloat16
    f32 = jnp.float32

    local_gram = lax.dot_general(
        item_table, item_table, (((0,), (0,)), ((), ())), preferred_element_type=f32
    )

    positions = lax.broadcasted_iota(jnp.int32, (user_count, history_length), 1)
    live = positions < counts[:, None]
    owners = histories // table_rows
    local_rows = histories - owners * table_rows
    owner_ids = lax.broadcasted_iota(jnp.int32, (user_count, history_length, devices), 2)
    by_owner = ((owners[:, :, None] == owner_ids) & live[:, :, None]).astype(bf16)
    per_user = jnp.sum(by_owner.astype(f32), axis=1)
    user_ids = lax.broadcasted_iota(jnp.int32, (user_count, user_count), 0)
    earlier_users = (lax.broadcasted_iota(jnp.int32, (user_count, user_count), 1) < user_ids).astype(bf16)
    before_user = jnp.einsum("uv,vo->uo", earlier_users, per_user.astype(bf16), preferred_element_type=f32)
    companions = jnp.concatenate([by_owner, before_user.astype(bf16)[:, None, :]], axis=1)
    same = jnp.einsum("ujo,uko->ujk", by_owner, companions, preferred_element_type=f32)
    slot_ids = lax.broadcasted_iota(jnp.int32, (history_length, history_length + 1), 0)
    other_ids = lax.broadcasted_iota(jnp.int32, (history_length, history_length + 1), 1)
    counted = ((other_ids < slot_ids) | (other_ids == history_length)).astype(f32)
    ranks = jnp.einsum("ujk,jk->uj", same, counted).astype(jnp.int32).reshape(lookups)

    flat_rows = local_rows.reshape(lookups, 1)
    row_high = flat_rows // 32
    row_low = flat_rows - row_high * 32
    user_of = lax.broadcasted_iota(jnp.int32, (user_count, history_length), 0).reshape(lookups, 1)
    flat_live = live.reshape(lookups, 1)
    columns = lax.broadcasted_iota(jnp.int32, (lookups, 4 * capacity), 1)
    part = columns // capacity
    chosen = (columns - part * capacity == ranks[:, None]) & flat_live
    value = jnp.where(
        part == 0, row_high, jnp.where(part == 1, row_low, jnp.where(part == 2, user_of, 1))
    )
    spread = jnp.where(chosen, value, 0).astype(bf16)
    slots = jnp.einsum(
        "io,ic->oc", by_owner.reshape(lookups, devices), spread, preferred_element_type=f32
    ).reshape(devices, 4, capacity)
    slots = slots.astype(jnp.int32)
    requests = slots[:, 0] * 32 + slots[:, 1]
    slot_user = slots[:, 2].reshape(slots_total)
    slot_used = slots[:, 3].reshape(slots_total)


    gram_width = embed_width * embed_width // devices
    outgoing = jnp.concatenate(
        [requests.astype(f32), local_gram.reshape(devices, gram_width)], axis=1
    )
    received = exchange(outgoing)
    incoming = received[:, :capacity].astype(jnp.int32).reshape(slots_total)
    gram_slice = jnp.sum(received[:, capacity:], axis=0)
    high = lax.optimization_barrier(gram_slice.astype(bf16))
    rest = gram_slice - high.astype(f32)
    middle = lax.optimization_barrier(rest.astype(bf16))
    low = (rest - middle.astype(f32)).astype(bf16)
    pieces = jnp.concatenate([high, middle, low], axis=0)
    extra_rows = -(-pieces.shape[0] // embed_width)
    pieces = jnp.pad(pieces, (0, extra_rows * embed_width - pieces.shape[0]))
    source_rows = jnp.concatenate(
        [item_table.astype(f32), pieces.astype(f32).reshape(extra_rows, embed_width)], axis=0
    )
    reply_capacity = capacity + extra_rows
    answered = answer_rows(source_rows, incoming, devices, reply_capacity, bf16)
    replies = exchange(answered)
    parts = replies[:, capacity:].reshape(devices, extra_rows * embed_width)[:, : 3 * gram_width]
    parts = parts.astype(f32).reshape(devices, 3, gram_width)
    gramian = ((parts[:, 0] + parts[:, 1]) + parts[:, 2]).reshape(embed_width, embed_width)
    reply_rows = replies.reshape(devices * reply_capacity, embed_width)
    slot_index = owners.reshape(lookups) * reply_capacity + ranks
    fetched = gather_rows(reply_rows.astype(f32), slot_index, bf16).reshape(
        user_count, history_length, embed_width
    )
    weights = live.astype(f32)
    narrow_weights = weights.astype(bf16)
    target = jnp.einsum("ul,ulk->uk", narrow_weights, fetched, preferred_element_type=f32)
    unseen_scale = unobserved_weight / (table_rows * devices)
    solution = jnp.zeros_like(target)
    residual = target
    direction = target
    norm_now = jnp.sum(residual * residual, axis=1)
    for iteration in range(ITERS):
        narrow = direction.astype(bf16)
        scores = jnp.einsum("ulk,uk->ul", fetched, narrow, preferred_element_type=f32)
        scores = (scores * weights).astype(bf16)
        returned = jnp.einsum("ulk,ul->uk", fetched, scores, preferred_element_type=f32)
        curved = jnp.dot(direction, gramian, precision=lax.Precision.HIGHEST)
        applied = unseen_scale * curved + returned + ridge * direction
        step_size = norm_now / jnp.sum(direction * applied, axis=1)
        solution = solution + step_size[:, None] * direction
        residual = residual - step_size[:, None] * applied
        norm_next = jnp.sum(residual * residual, axis=1)
        direction = residual + (norm_next / norm_now)[:, None] * direction
        norm_now = norm_next

    member_ids = lax.broadcasted_iota(jnp.int32, (slots_total, user_count), 1)
    member = ((slot_user[:, None] == member_ids) & (slot_used[:, None] > 0)).astype(bf16)
    partials = jnp.einsum("su,uk->sk", member, solution.astype(bf16), preferred_element_type=f32)
    partials = partials.astype(bf16).reshape(devices, capacity, embed_width)
    arrived = exchange(partials).reshape(slots_total, embed_width)
    table_ids = lax.broadcasted_iota(jnp.int32, (slots_total, table_rows), 1)
    picks = (incoming[:, None] == table_ids).astype(bf16)
    item_rhs = jnp.einsum("st,sk->tk", picks, arrived, preferred_element_type=f32)
    return (solution, item_rhs)


def solution(mesh):
    return jax.shard_map(
        on_device,
        mesh=mesh,
        in_specs=(P(("rows", "grp"), None), P(("rows", "grp"), None), P(("rows", "grp"))),
        out_specs=(P(("rows", "grp"), None), P(("rows", "grp"), None)),
        check_vma=False,
    )
```
